32 devices in a mesh: region: 4 (over z), narrow: 8 (over y, x, core).
Axes of the slice: x: 2, y: 2, z: 4, core: 2. Of those that a mesh axis runs over, the one named last changes fastest.
Arguments:
- dust_pos: float32 [3, 6144], P(None, ('region', 'narrow')), may hold values from -1 to 1
- dust_vel: float32 [3, 6144], P(None, ('region', 'narrow')), may hold values from -6 to 6
- dust_tau: float32 [6144], P(('region', 'narrow')), may hold values from 0.02 to 2
- dest: int32 [6144, 1], P(('region', 'narrow')), may hold values from 0 to 3; in each aligned block of 192 rows (0 to 191, 192 to 383, ...) at most 96 rows name the same one
- counts: int32 [32], P(('region', 'narrow')), may hold values from 96 to 192, as said below
- wake_pos: float32 [3, 32768], P(None, ('region', 'narrow')), may hold values from -1 to 1
- wake_gamma: float32 [3, 32768], P(None, ('region', 'narrow')), may hold values from -0.3 to 0.3
- wake_core: float32 [32768], P(('region', 'narrow')), may hold values from 0.05 to 0.3
Outputs:
- moved: float32 [6, 12288], P(None, ('region', 'narrow'))
The draws below stay inside these ranges and needn't reach their ends.
Inputs may be any that keep to these rules, and one draw needn't show every extreme that they name: `dest`: in each device's 192 rows, no region is named by more than 96 rows, and some device's rows name some region exactly 96 times. `counts`: some device has all its rows live in every draw.
All inputs are finite; a program needn't handle non-finite values.
Results may differ from the reference program's by a relative error of at most 0.0003.
Values sent between devices are 32-bit elements; how exact they have to be, the bound alone decides.
No kernel may reach another device: no remote copies, remote signals or barrier semaphores. Data moves between devices by JAX's collectives and lax.ppermute only.
A program may use at most 64 MiB of HBM per device.

```python
import math
import jax
import jax.numpy as jnp
import numpy as np
from jax import lax

DUST_DEV = 192
WAKE_DEV = 1024
CAP = 96
SLOTS_DEV = 384
DUST = 6144
NWAKE = 32768
TOTAL_SLOTS = 12288
N_REGION = 4
N_NARROW = 8


def draw_counts(key, part):
    device_count = N_REGION * N_NARROW
    first_key, second_key = jax.random.split(jax.random.fold_in(key, 17))
    base_counts = jax.random.randint(first_key, (device_count,), DUST_DEV // 2, DUST_DEV + 1)
    full_device = jax.random.randint(second_key, (), 0, device_count)
    chosen = jnp.arange(device_count, dtype=jnp.int32) == full_device
    return jnp.where(chosen, DUST_DEV, base_counts).astype(jnp.int32)


def shard_levels(rng, dims, pieces, low, high):
    factor_of = 1.0
    for dim, blocks in pieces:
        draws = jax.random.uniform(jax.random.fold_in(jax.random.fold_in(rng, 6), dim), (blocks,), jnp.float32, low / len(pieces), high / len(pieces))
        factor_of = factor_of * jnp.repeat(jnp.exp(draws), dims[dim] // blocks).reshape((-1,) + (1,) * (len(dims) - 1 - dim))
    return factor_of


def shared_out(stream_key, own, number, rows, number_of, top, limit, skew):
    ranking = jax.random.permutation(stream_key, number_of)
    crowded, ordinary = load_shares(number_of, rows * top, limit, skew, True), load_shares(number_of, rows * top, limit, skew, False)
    places = jnp.arange(number_of)

    def named(tallies, rotation):
        used = int((tallies > 0).sum())
        fixed = max(1, used // 4)
        shifted = fixed + (places - fixed + rotation * (used - fixed)) % max(1, number_of - fixed)
        return jnp.zeros((number_of,), jnp.int32).at[ranking[jnp.where(places < fixed, places, shifted)]].set(jnp.asarray(tallies, jnp.int32))

    tallies = jnp.where(number % 4 == 0, named(crowded, number // 4), named(ordinary, number - number // 4 - 1))
    mixed = jax.random.permutation(jax.random.fold_in(own, 3), number_of)
    donor, sink = mixed[0:number_of // 2 * 2:2], mixed[1:number_of // 2 * 2:2]
    slack = jnp.minimum(tallies[donor] - 1, limit - tallies[sink]) // 2
    slack = jnp.where((donor == ranking[0]) | (sink == ranking[0]) | (tallies[sink] == 0), 0, jnp.maximum(slack, 0))
    shifted = jax.random.randint(jax.random.fold_in(own, 4), (number_of // 2,), 0, 1 << 20) % (slack + 1)
    tallies = tallies.at[donor].add(-shifted).at[sink].add(shifted)
    labels = jnp.searchsorted(jnp.cumsum(tallies), jnp.arange(rows * top), side="right").astype(jnp.int32)
    listing = labels.reshape(top, rows).T
    listing = listing[jax.random.permutation(jax.random.fold_in(own, 1), rows)]
    rotation = jax.random.randint(jax.random.fold_in(own, 2), (rows, 1), 0, top)
    return jnp.take_along_axis(listing, (jnp.arange(top)[None, :] + rotation) % top, axis=1)


def load_shares(number_of, total, reach, skew, full):
    weights = [(1 << 20) // math.isqrt(grade ** skew) + 1 for grade in range(1, number_of + 1)]
    largest = reach if full else min(reach, max(-(-total // number_of), total * weights[0] // sum(weights)))
    least = 1 if total - largest >= number_of - 1 else 0
    holding, spare = [largest] + [least] * (number_of - 1), total - largest - least * (number_of - 1)
    while spare > 0:
        candidates = [i for i in range(1, number_of) if holding[i] < largest] or [i for i in range(1, number_of) if holding[i] < reach]
        mass, left = sum([weights[i] for i in candidates]), spare
        for i in candidates:
            more = min(reach - holding[i], max(1, left * weights[i] // mass), spare)
            holding[i] = holding[i] + more
            spare = spare - more
    return np.array(holding)


def normal_values(own_key, dims, spread, bound, pieces=(), held_as=jnp.bfloat16):
    gain = shard_levels(own_key, dims, pieces, -0.22, 0.18) if pieces else 1.0
    entries = jax.random.normal(own_key, dims, jnp.float32) * spread * gain
    return jnp.minimum(jnp.maximum(entries, -bound), bound).astype(held_as)


def setup_inputs(seed: int = 0) -> dict:
    keys = jax.random.split(jax.random.key(seed), 9)
    dust_pos = jnp.clip(jax.random.uniform(keys[0], (3, DUST), jnp.float32, -1.0, 1.0) * shard_levels(keys[0], (3, DUST), ((1, 32),), -0.4, 0.0), -1.0, 1.0)
    dust_vel = normal_values(keys[1], (3, DUST), 1.0, 6.0, ((1, 32),), jnp.float32)
    dust_tau = jnp.clip(jnp.exp(math.log(2.0) - 4.6051702 * jax.random.uniform(keys[2], (DUST,), jnp.float32) ** shard_levels(keys[2], (DUST,), ((0, 32),), -0.2, 0.2)), 0.02, 2.0)
    dest_keys = jax.random.split(jax.random.fold_in(keys[3], 1), DUST // DUST_DEV)
    dest_turns = jax.random.permutation(jax.random.fold_in(keys[3], 3), DUST // DUST_DEV)
    dest = jax.vmap(lambda own, number: shared_out(jax.random.fold_in(keys[3], 2), own, number, DUST_DEV, N_REGION, 1, CAP, 2))(dest_keys, dest_turns).reshape((DUST, 1))
    counts = draw_counts(jax.random.fold_in(keys[8], 71), 0)
    wake_pos = jnp.clip(jax.random.uniform(keys[5], (3, NWAKE), jnp.float32, -1.0, 1.0) * shard_levels(keys[5], (3, NWAKE), ((1, 32),), -0.4, 0.0), -1.0, 1.0)
    wake_gamma = normal_values(keys[6], (3, NWAKE), 0.05, 0.3, ((1, 32),), jnp.float32)
    wake_core = jnp.clip(jnp.exp(math.log(0.3) - 1.7917595 * jax.random.uniform(keys[7], (NWAKE,), jnp.float32) ** shard_levels(keys[7], (NWAKE,), ((0, 32),), -0.2, 0.2)), 0.05, 0.3)
    return {"dust_pos": dust_pos, "dust_vel": dust_vel, "dust_tau": dust_tau, "dest": dest, "counts": counts, "wake_pos": wake_pos, "wake_gamma": wake_gamma, "wake_core": wake_core}


step_size = 0.1
gravity = 1.0

def cross_rows(first, second):
    return jnp.stack([first[1] * second[2] - first[2] * second[1], first[2] * second[0] - first[0] * second[2], first[0] * second[1] - first[1] * second[0]])

def raw_terms(points, wake_block):
    point_count = points.shape[1]
    wake_count = wake_block.shape[1]
    point_width = point_count if point_count <= 2048 else math.gcd(point_count, 2048)
    wake_width = math.gcd(wake_count, 2048)
    wake_place = wake_block[0:3]
    vortex_gamma = wake_block[3:6]
    core_square = wake_block[6] * wake_block[6]
    tables = jnp.concatenate([vortex_gamma, cross_rows(vortex_gamma, wake_place)], axis=0)
    place_blocks = wake_place.reshape(3, wake_count // wake_width, wake_width).transpose(1, 0, 2)
    table_blocks = tables.reshape(6, wake_count // wake_width, wake_width).transpose(1, 0, 2)
    core_blocks = core_square.reshape(wake_count // wake_width, wake_width)
    point_blocks = points.reshape(3, point_count // point_width, point_width).transpose(1, 0, 2)

    def one_block(point_group):

        def accumulate(running, parts):
            place_part, table_part, core_part = parts
            first_gap = point_group[0][:, None] - place_part[0][None, :]
            second_gap = point_group[1][:, None] - place_part[1][None, :]
            third_gap = point_group[2][:, None] - place_part[2][None, :]
            distance_sq = first_gap * first_gap + second_gap * second_gap + third_gap * third_gap + core_part[None, :]
            kernel = 1.0 / (distance_sq * jnp.sqrt(distance_sq))
            product = lax.dot_general(table_part, kernel, (((1,), (1,)), ((), ())), precision=lax.Precision.HIGHEST)
            return (running + product, None)
        total, _ = lax.scan(accumulate, jnp.zeros((6, point_width), jnp.float32), (place_blocks, table_blocks, core_blocks))
        return total
    result = lax.map(one_block, point_blocks)
    return result.transpose(1, 0, 2).reshape(6, point_count)

def advance(arrived, raw_sums):
    points = arrived[0:3]
    velocity = arrived[3:6]
    live_flag = arrived[7]
    wind = (cross_rows(raw_sums[0:3], points) - raw_sums[3:6]) / (4.0 * math.pi)
    safe_tau = jnp.where(live_flag > 0.5, arrived[6], 1.0)
    rate = step_size / safe_tau
    upward = jnp.array([0.0, 0.0, 1.0], jnp.float32)[:, None]
    new_velocity = (velocity + rate[None, :] * wind - step_size * gravity * upward) / (1.0 + rate[None, :])
    new_place = points + step_size * new_velocity
    return jnp.concatenate([new_place, new_velocity], axis=0) * live_flag[None, :]

def reference(dust_pos, dust_vel, dust_tau, dest, counts, wake_pos, wake_gamma, wake_core):
    device_count = N_REGION * N_NARROW
    target = dest[:, 0].reshape(device_count, DUST_DEV)
    row_index = jnp.arange(DUST_DEV, dtype=jnp.int32)
    live_rows = (row_index[None, :] < counts[:, None]).astype(jnp.float32).reshape(-1)
    onehot = (target[:, :, None] == jnp.arange(N_REGION, dtype=jnp.int32)[None, None, :]).astype(jnp.int32)
    slot_rank = lax.optimization_barrier(jnp.sum((jnp.cumsum(onehot, axis=1) - onehot) * onehot, axis=2))
    device_index = jnp.arange(device_count, dtype=jnp.int32)
    source_region = device_index // N_NARROW
    source_lane = device_index % N_NARROW
    column = ((target * N_NARROW + source_lane[:, None]) * SLOTS_DEV + source_region[:, None] * CAP + slot_rank).reshape(-1).astype(jnp.int32)
    dust_state = jnp.concatenate([dust_pos, dust_vel, dust_tau[None, :], jnp.ones((1, DUST), jnp.float32)], axis=0) * live_rows[None, :]
    slots = jnp.zeros((8, TOTAL_SLOTS), jnp.float32).at[:, column].add(dust_state)
    wake_rows = jnp.concatenate([wake_pos, wake_gamma, wake_core[None, :]], axis=0)

    def per_device(target_device):
        region_index = target_device // N_NARROW
        points = lax.dynamic_slice_in_dim(slots[0:3], (target_device * SLOTS_DEV).astype(jnp.int32), SLOTS_DEV, 1)
        region_wake = lax.dynamic_slice_in_dim(wake_rows, (region_index * N_NARROW * WAKE_DEV).astype(jnp.int32), N_NARROW * WAKE_DEV, 1)
        return raw_terms(points, region_wake)
    raw_all = lax.map(per_device, device_index)
    raw_sums = raw_all.transpose(1, 0, 2).reshape(6, TOTAL_SLOTS)
    return advance(slots, raw_sums)
```

```python
import math

import jax
import jax.numpy as jnp
from jax import lax
from jax.sharding import PartitionSpec as P

step_size = 0.1
gravity = 1.0


def cross_rows(first, second):
    return jnp.stack(
        [
            first[1] * second[2] - first[2] * second[1],
            first[2] * second[0] - first[0] * second[2],
            first[0] * second[1] - first[1] * second[0],
        ]
    )


def raw_terms(points, wake_block):
    point_count = points.shape[1]
    wake_count = wake_block.shape[1]
    wake_width = math.gcd(wake_count, 2048)
    wake_place = wake_block[0:3]
    vortex_gamma = wake_block[3:6]
    core_square = wake_block[6] * wake_block[6]
    tables = jnp.concatenate([vortex_gamma, cross_rows(vortex_gamma, wake_place)], axis=0)
    place_blocks = wake_place.reshape(3, wake_count // wake_width, wake_width).transpose(1, 0, 2)
    table_blocks = tables.reshape(6, wake_count // wake_width, wake_width).transpose(1, 0, 2)
    core_blocks = core_square.reshape(wake_count // wake_width, wake_width)
    point_blocks = points.reshape(3, point_count // point_count, point_count).transpose(1, 0, 2)

    def one_block(point_group):

        def accumulate(running, parts):
            place_part, table_part, core_part = parts
            first_gap = point_group[0][:, None] - place_part[0][None, :]
            second_gap = point_group[1][:, None] - place_part[1][None, :]
            third_gap = point_group[2][:, None] - place_part[2][None, :]
            distance_sq = (
                first_gap * first_gap
                + second_gap * second_gap
                + third_gap * third_gap
                + core_part[None, :]
            )
            kernel = 1.0 / (distance_sq * jnp.sqrt(distance_sq))
            product = lax.dot_general(
                table_part, kernel, (((1,), (1,)), ((), ())), precision=lax.Precision.HIGHEST
            )
            return (running + product, None)

        total, _ = lax.scan(
            accumulate,
            jnp.zeros((6, point_count), jnp.float32),
            (place_blocks, table_blocks, core_blocks),
        )
        return total

    result = lax.map(one_block, point_blocks)
    return result.transpose(1, 0, 2).reshape(6, point_count)


def advance(arrived, raw_sums):
    points = arrived[0:3]
    velocity = arrived[3:6]
    live_flag = arrived[7]
    wind = (cross_rows(raw_sums[0:3], points) - raw_sums[3:6]) / (4.0 * math.pi)
    safe_tau = jnp.where(live_flag > 0.5, arrived[6], 1.0)
    rate = step_size / safe_tau
    upward = jnp.array([0.0, 0.0, 1.0], jnp.float32)[:, None]
    new_velocity = (velocity + rate[None, :] * wind - step_size * gravity * upward) / (
        1.0 + rate[None, :]
    )
    new_place = points + step_size * new_velocity
    return jnp.concatenate([new_place, new_velocity], axis=0) * live_flag[None, :]


def gather_wake(wake_rows):
    lanes = lax.axis_size("narrow")
    if lanes > 8:
        return lax.all_gather(wake_rows, "narrow", axis=1, tiled=True)
    parts = [wake_rows]
    for shift in range(1, lanes):
        pairs = [(i, (i + shift) % lanes) for i in range(lanes)]
        parts.append(lax.ppermute(wake_rows, "narrow", pairs))
    return jnp.concatenate(parts, axis=1)


def exchange_slots(outgoing, capacity):
    regions = lax.axis_size("region")
    if regions > 8:
        return lax.all_to_all(outgoing, "region", split_axis=1, concat_axis=1, tiled=True)
    region = lax.axis_index("region")
    blocks = outgoing.reshape(outgoing.shape[0], regions, capacity)
    by_shift = [jnp.take(blocks, region, axis=1)]
    for shift in range(1, regions):
        pairs = [(i, (i + shift) % regions) for i in range(regions)]
        sent = jnp.take(blocks, (region + shift) % regions, axis=1)
        by_shift.append(lax.ppermute(sent, "region", pairs))
    stacked = jnp.stack(by_shift, axis=1)
    order = (region - jnp.arange(regions, dtype=jnp.int32)) % regions
    return jnp.take(stacked, order, axis=1).reshape(outgoing.shape[0], regions * capacity)


def body(dust_pos, dust_vel, dust_tau, dest, counts, wake_pos, wake_gamma, wake_core):
    per_device = dust_tau.shape[0]
    regions = lax.axis_size("region")
    capacity = 2 * per_device // regions
    slot_count = regions * capacity
    wake_rows = jnp.concatenate([wake_pos, wake_gamma, wake_core[None, :]], axis=0)
    region_wake = gather_wake(wake_rows)
    live_rows = (jnp.arange(per_device, dtype=jnp.int32) < counts[0]).astype(jnp.float32)
    target = dest[:, 0]
    row = jnp.arange(per_device, dtype=jnp.int32)
    earlier = (target[:, None] == target[None, :]) & (row[None, :] < row[:, None])
    slot_rank = jnp.sum(earlier.astype(jnp.int32), axis=1)
    column = target * capacity + slot_rank
    placing = (column[:, None] == jnp.arange(slot_count, dtype=jnp.int32)[None, :]).astype(
        jnp.float32
    )
    dust_state = (
        jnp.concatenate(
            [dust_pos, dust_vel, dust_tau[None, :], jnp.ones((1, per_device), jnp.float32)], axis=0
        )
        * live_rows[None, :]
    )
    outgoing = jnp.dot(
        dust_state, placing, precision=lax.Precision.HIGHEST, preferred_element_type=jnp.float32
    )
    arrived = exchange_slots(outgoing, capacity)
    points = arrived[0:3]
    raw_sums = raw_terms(points, region_wake)
    return advance(arrived, raw_sums)


def solution(mesh):
    in_specs = (
        P(None, ("region", "narrow")),
        P(None, ("region", "narrow")),
        P(("region", "narrow")),
        P(("region", "narrow"), None),
        P(("region", "narrow")),
        P(None, ("region", "narrow")),
        P(None, ("region", "narrow")),
        P(("region", "narrow")),
    )
    out_specs = P(None, ("region", "narrow"))
    return jax.shard_map(body, mesh=mesh, in_specs=in_specs, out_specs=out_specs, check_vma=False)
```

```python
import math

import jax
import jax.numpy as jnp
from jax import lax
from jax.sharding import PartitionSpec as P

step_size = 0.1
gravity = 1.0


def cross_rows(first, second):
    return jnp.stack(
        [
            first[1] * second[2] - first[2] * second[1],
            first[2] * second[0] - first[0] * second[2],
            first[0] * second[1] - first[1] * second[0],
        ]
    )


def raw_terms(points, wake_block):
    point_count = points.shape[1]
    wake_count = wake_block.shape[1]
    wake_width = math.gcd(wake_count, 2048)
    wake_place = wake_block[0:3]
    vortex_gamma = wake_block[3:6]
    core_square = wake_block[6] * wake_block[6]
    tables = jnp.concatenate([vortex_gamma, cross_rows(vortex_gamma, wake_place)], axis=0)
    place_blocks = wake_place.reshape(3, wake_count // wake_width, wake_width).transpose(1, 0, 2)
    table_blocks = tables.reshape(6, wake_count // wake_width, wake_width).transpose(1, 0, 2)
    core_blocks = core_square.reshape(wake_count // wake_width, wake_width)
    point_blocks = points.reshape(3, point_count // point_count, point_count).transpose(1, 0, 2)

    def one_block(point_group):

        def accumulate(running, parts):
            place_part, table_part, core_part = parts
            first_gap = point_group[0][:, None] - place_part[0][None, :]
            second_gap = point_group[1][:, None] - place_part[1][None, :]
            third_gap = point_group[2][:, None] - place_part[2][None, :]
            distance_sq = (
                first_gap * first_gap
                + second_gap * second_gap
                + third_gap * third_gap
                + core_part[None, :]
            )
            kernel = 1.0 / (distance_sq * jnp.sqrt(distance_sq))
            product = lax.dot_general(
                table_part, kernel, (((1,), (1,)), ((), ())), precision=lax.Precision.HIGHEST
            )
            return (running + product, None)

        total, _ = lax.scan(
            accumulate,
            jnp.zeros((6, point_count), jnp.float32),
            (place_blocks, table_blocks, core_blocks),
        )
        return total

    result = lax.map(one_block, point_blocks)
    return result.transpose(1, 0, 2).reshape(6, point_count)


def advance(arrived, raw_sums):
    points = arrived[0:3]
    velocity = arrived[3:6]
    live_flag = arrived[7]
    wind = (cross_rows(raw_sums[0:3], points) - raw_sums[3:6]) / (4.0 * math.pi)
    safe_tau = jnp.where(live_flag > 0.5, arrived[6], 1.0)
    rate = step_size / safe_tau
    upward = jnp.array([0.0, 0.0, 1.0], jnp.float32)[:, None]
    new_velocity = (velocity + rate[None, :] * wind - step_size * gravity * upward) / (
        1.0 + rate[None, :]
    )
    new_place = points + step_size * new_velocity
    return jnp.concatenate([new_place, new_velocity], axis=0) * live_flag[None, :]


def exchange_slots(outgoing, capacity):
    regions = lax.axis_size("region")
    if regions > 8:
        return lax.all_to_all(outgoing, "region", split_axis=1, concat_axis=1, tiled=True)
    region = lax.axis_index("region")
    blocks = outgoing.reshape(outgoing.shape[0], regions, capacity)
    by_shift = [jnp.take(blocks, region, axis=1)]
    for shift in range(1, regions):
        pairs = [(i, (i + shift) % regions) for i in range(regions)]
        sent = jnp.take(blocks, (region + shift) % regions, axis=1)
        by_shift.append(lax.ppermute(sent, "region", pairs))
    stacked = jnp.stack(by_shift, axis=1)
    order = (region - jnp.arange(regions, dtype=jnp.int32)) % regions
    return jnp.take(stacked, order, axis=1).reshape(outgoing.shape[0], regions * capacity)


def body(dust_pos, dust_vel, dust_tau, dest, counts, wake_pos, wake_gamma, wake_core):
    per_device = dust_tau.shape[0]
    regions = lax.axis_size("region")
    capacity = 2 * per_device // regions
    slot_count = regions * capacity
    live_rows = (jnp.arange(per_device, dtype=jnp.int32) < counts[0]).astype(jnp.float32)
    target = dest[:, 0]
    row = jnp.arange(per_device, dtype=jnp.int32)
    earlier = (target[:, None] == target[None, :]) & (row[None, :] < row[:, None])
    slot_rank = jnp.sum(earlier.astype(jnp.int32), axis=1)
    column = target * capacity + slot_rank
    placing = (column[:, None] == jnp.arange(slot_count, dtype=jnp.int32)[None, :]).astype(
        jnp.float32
    )
    dust_state = (
        jnp.concatenate(
            [dust_pos, dust_vel, dust_tau[None, :], jnp.ones((1, per_device), jnp.float32)], axis=0
        )
        * live_rows[None, :]
    )
    outgoing = jnp.dot(
        dust_state, placing, precision=lax.Precision.HIGHEST, preferred_element_type=jnp.float32
    )
    wake_rows = jnp.concatenate([wake_pos, wake_gamma, wake_core[None, :]], axis=0)
    outgoing, wake_rows = lax.optimization_barrier((outgoing, wake_rows))
    arrived = exchange_slots(outgoing, capacity)
    region_wake = lax.all_gather(wake_rows, "narrow", axis=1, tiled=True)
    points = arrived[0:3]
    raw_sums = raw_terms(points, region_wake)
    return advance(arrived, raw_sums)


def solution(mesh):
    in_specs = (
        P(None, ("region", "narrow")),
        P(None, ("region", "narrow")),
        P(("region", "narrow")),
        P(("region", "narrow"), None),
        P(("region", "narrow")),
        P(None, ("region", "narrow")),
        P(None, ("region", "narrow")),
        P(("region", "narrow")),
    )
    out_specs = P(None, ("region", "narrow"))
    return jax.shard_map(body, mesh=mesh, in_specs=in_specs, out_specs=out_specs, check_vma=False)
```

```python
import math

import jax
import jax.numpy as jnp
from jax import lax
from jax.sharding import PartitionSpec as P

step_size = 0.1
gravity = 1.0


def cross_rows(first, second):
    return jnp.stack(
        [
            first[1] * second[2] - first[2] * second[1],
            first[2] * second[0] - first[0] * second[2],
            first[0] * second[1] - first[1] * second[0],
        ]
    )


def raw_terms(points, wake_block):
    point_count = points.shape[1]
    wake_count = wake_block.shape[1]
    wake_width = math.gcd(wake_count, 2048)
    wake_place = wake_block[0:3]
    vortex_gamma = wake_block[3:6]
    core_square = wake_block[6] * wake_block[6]
    tables = jnp.concatenate([vortex_gamma, cross_rows(vortex_gamma, wake_place)], axis=0)
    place_blocks = wake_place.reshape(3, wake_count // wake_width, wake_width).transpose(1, 0, 2)
    table_blocks = tables.reshape(6, wake_count // wake_width, wake_width).transpose(1, 0, 2)
    core_blocks = core_square.reshape(wake_count // wake_width, wake_width)
    point_blocks = points.reshape(3, point_count // point_count, point_count).transpose(1, 0, 2)

    def one_block(point_group):

        def accumulate(running, parts):
            place_part, table_part, core_part = parts
            first_gap = point_group[0][:, None] - place_part[0][None, :]
            second_gap = point_group[1][:, None] - place_part[1][None, :]
            third_gap = point_group[2][:, None] - place_part[2][None, :]
            distance_sq = (
                first_gap * first_gap
                + second_gap * second_gap
                + third_gap * third_gap
                + core_part[None, :]
            )
            kernel = 1.0 / (distance_sq * jnp.sqrt(distance_sq))
            product = lax.dot_general(
                table_part, kernel, (((1,), (1,)), ((), ())), precision=lax.Precision.HIGH
            )
            return (running + product, None)

        total, _ = lax.scan(
            accumulate,
            jnp.zeros((6, point_count), jnp.float32),
            (place_blocks, table_blocks, core_blocks),
        )
        return total

    result = lax.map(one_block, point_blocks)
    return result.transpose(1, 0, 2).reshape(6, point_count)


def advance(arrived, raw_sums):
    points = arrived[0:3]
    velocity = arrived[3:6]
    live_flag = arrived[7]
    wind = (cross_rows(raw_sums[0:3], points) - raw_sums[3:6]) / (4.0 * math.pi)
    safe_tau = jnp.where(live_flag > 0.5, arrived[6], 1.0)
    rate = step_size / safe_tau
    upward = jnp.array([0.0, 0.0, 1.0], jnp.float32)[:, None]
    new_velocity = (velocity + rate[None, :] * wind - step_size * gravity * upward) / (
        1.0 + rate[None, :]
    )
    new_place = points + step_size * new_velocity
    return jnp.concatenate([new_place, new_velocity], axis=0) * live_flag[None, :]


def exchange_slots(outgoing, capacity):
    regions = lax.axis_size("region")
    if regions > 8:
        return lax.all_to_all(outgoing, "region", split_axis=1, concat_axis=1, tiled=True)
    region = lax.axis_index("region")
    blocks = outgoing.reshape(outgoing.shape[0], regions, capacity)
    by_shift = [jnp.take(blocks, region, axis=1)]
    for shift in range(1, regions):
        pairs = [(i, (i + shift) % regions) for i in range(regions)]
        sent = jnp.take(blocks, (region + shift) % regions, axis=1)
        by_shift.append(lax.ppermute(sent, "region", pairs))
    stacked = jnp.stack(by_shift, axis=1)
    order = (region - jnp.arange(regions, dtype=jnp.int32)) % regions
    return jnp.take(stacked, order, axis=1).reshape(outgoing.shape[0], regions * capacity)


def body(dust_pos, dust_vel, dust_tau, dest, counts, wake_pos, wake_gamma, wake_core):
    per_device = dust_tau.shape[0]
    regions = lax.axis_size("region")
    capacity = 2 * per_device // regions
    slot_count = regions * capacity
    live_rows = (jnp.arange(per_device, dtype=jnp.int32) < counts[0]).astype(jnp.float32)
    target = dest[:, 0]
    row = jnp.arange(per_device, dtype=jnp.int32)
    earlier = (target[:, None] == target[None, :]) & (row[None, :] < row[:, None])
    slot_rank = jnp.sum(earlier.astype(jnp.int32), axis=1)
    column = target * capacity + slot_rank
    placing = (column[:, None] == jnp.arange(slot_count, dtype=jnp.int32)[None, :]).astype(
        jnp.float32
    )
    dust_state = (
        jnp.concatenate(
            [dust_pos, dust_vel, dust_tau[None, :], jnp.ones((1, per_device), jnp.float32)], axis=0
        )
        * live_rows[None, :]
    )
    outgoing = jnp.dot(
        dust_state, placing, precision=lax.Precision.HIGHEST, preferred_element_type=jnp.float32
    )
    wake_rows = jnp.concatenate([wake_pos, wake_gamma, wake_core[None, :]], axis=0)
    outgoing, wake_rows = lax.optimization_barrier((outgoing, wake_rows))
    arrived = exchange_slots(outgoing, capacity)
    region_wake = lax.all_gather(wake_rows, "narrow", axis=1, tiled=True)
    points = arrived[0:3]
    raw_sums = raw_terms(points, region_wake)
    return advance(arrived, raw_sums)


def solution(mesh):
    in_specs = (
        P(None, ("region", "narrow")),
        P(None, ("region", "narrow")),
        P(("region", "narrow")),
        P(("region", "narrow"), None),
        P(("region", "narrow")),
        P(None, ("region", "narrow")),
        P(None, ("region", "narrow")),
        P(("region", "narrow")),
    )
    out_specs = P(None, ("region", "narrow"))
    return jax.shard_map(body, mesh=mesh, in_specs=in_specs, out_specs=out_specs, check_vma=False)
```

```python
import math

import jax
import jax.numpy as jnp
from jax import lax
from jax.sharding import PartitionSpec as P

step_size = 0.1
gravity = 1.0


def cross_rows(first, second):
    return jnp.stack(
        [
            first[1] * second[2] - first[2] * second[1],
            first[2] * second[0] - first[0] * second[2],
            first[0] * second[1] - first[1] * second[0],
        ]
    )


def raw_terms(points, wake_block):
    point_count = points.shape[1]
    wake_count = wake_block.shape[1]
    wake_width = math.gcd(wake_count, 2048)
    wake_place = wake_block[0:3]
    vortex_gamma = wake_block[3:6]
    core_square = wake_block[6] * wake_block[6]
    tables = jnp.concatenate([vortex_gamma, cross_rows(vortex_gamma, wake_place)], axis=0)
    place_blocks = wake_place.reshape(3, wake_count // wake_width, wake_width).transpose(1, 0, 2)
    table_blocks = tables.reshape(6, wake_count // wake_width, wake_width).transpose(1, 0, 2)
    core_blocks = core_square.reshape(wake_count // wake_width, wake_width)
    point_blocks = points.reshape(3, point_count // point_count, point_count).transpose(1, 0, 2)

    def one_block(point_group):

        def accumulate(running, parts):
            place_part, table_part, core_part = parts
            first_gap = point_group[0][:, None] - place_part[0][None, :]
            second_gap = point_group[1][:, None] - place_part[1][None, :]
            third_gap = point_group[2][:, None] - place_part[2][None, :]
            distance_sq = (
                first_gap * first_gap
                + second_gap * second_gap
                + third_gap * third_gap
                + core_part[None, :]
            )
            inverse_root = lax.rsqrt(distance_sq)
            kernel = inverse_root * inverse_root * inverse_root
            product = lax.dot_general(
                table_part, kernel, (((1,), (1,)), ((), ())), precision=lax.Precision.HIGH
            )
            return (running + product, None)

        total, _ = lax.scan(
            accumulate,
            jnp.zeros((6, point_count), jnp.float32),
            (place_blocks, table_blocks, core_blocks),
        )
        return total

    result = lax.map(one_block, point_blocks)
    return result.transpose(1, 0, 2).reshape(6, point_count)


def advance(arrived, raw_sums):
    points = arrived[0:3]
    velocity = arrived[3:6]
    live_flag = arrived[7]
    wind = (cross_rows(raw_sums[0:3], points) - raw_sums[3:6]) / (4.0 * math.pi)
    safe_tau = jnp.where(live_flag > 0.5, arrived[6], 1.0)
    rate = step_size / safe_tau
    upward = jnp.array([0.0, 0.0, 1.0], jnp.float32)[:, None]
    new_velocity = (velocity + rate[None, :] * wind - step_size * gravity * upward) / (
        1.0 + rate[None, :]
    )
    new_place = points + step_size * new_velocity
    return jnp.concatenate([new_place, new_velocity], axis=0) * live_flag[None, :]


def exchange_slots(outgoing, capacity):
    regions = lax.axis_size("region")
    if regions > 8:
        return lax.all_to_all(outgoing, "region", split_axis=1, concat_axis=1, tiled=True)
    region = lax.axis_index("region")
    blocks = outgoing.reshape(outgoing.shape[0], regions, capacity)
    by_shift = [jnp.take(blocks, region, axis=1)]
    for shift in range(1, regions):
        pairs = [(i, (i + shift) % regions) for i in range(regions)]
        sent = jnp.take(blocks, (region + shift) % regions, axis=1)
        by_shift.append(lax.ppermute(sent, "region", pairs))
    stacked = jnp.stack(by_shift, axis=1)
    order = (region - jnp.arange(regions, dtype=jnp.int32)) % regions
    return jnp.take(stacked, order, axis=1).reshape(outgoing.shape[0], regions * capacity)


def body(dust_pos, dust_vel, dust_tau, dest, counts, wake_pos, wake_gamma, wake_core):
    per_device = dust_tau.shape[0]
    regions = lax.axis_size("region")
    capacity = 2 * per_device // regions
    slot_count = regions * capacity
    live_rows = (jnp.arange(per_device, dtype=jnp.int32) < counts[0]).astype(jnp.float32)
    target = dest[:, 0]
    row = jnp.arange(per_device, dtype=jnp.int32)
    earlier = (target[:, None] == target[None, :]) & (row[None, :] < row[:, None])
    slot_rank = jnp.sum(earlier.astype(jnp.int32), axis=1)
    column = target * capacity + slot_rank
    placing = (column[:, None] == jnp.arange(slot_count, dtype=jnp.int32)[None, :]).astype(
        jnp.float32
    )
    dust_state = (
        jnp.concatenate(
            [dust_pos, dust_vel, dust_tau[None, :], jnp.ones((1, per_device), jnp.float32)], axis=0
        )
        * live_rows[None, :]
    )
    outgoing = jnp.dot(
        dust_state, placing, precision=lax.Precision.HIGHEST, preferred_element_type=jnp.float32
    )
    wake_rows = jnp.concatenate([wake_pos, wake_gamma, wake_core[None, :]], axis=0)
    outgoing, wake_rows = lax.optimization_barrier((outgoing, wake_rows))
    arrived = exchange_slots(outgoing, capacity)
    region_wake = lax.all_gather(wake_rows, "narrow", axis=1, tiled=True)
    points = arrived[0:3]
    raw_sums = raw_terms(points, region_wake)
    return advance(arrived, raw_sums)


def solution(mesh):
    in_specs = (
        P(None, ("region", "narrow")),
        P(None, ("region", "narrow")),
        P(("region", "narrow")),
        P(("region", "narrow"), None),
        P(("region", "narrow")),
        P(None, ("region", "narrow")),
        P(None, ("region", "narrow")),
        P(("region", "narrow")),
    )
    out_specs = P(None, ("region", "narrow"))
    return jax.shard_map(body, mesh=mesh, in_specs=in_specs, out_specs=out_specs, check_vma=False)
```

```python
import functools
import math

import jax
import jax.numpy as jnp
from jax import lax
from jax.experimental import pallas as pl
from jax.experimental.pallas import tpu as pltpu
from jax.sharding import PartitionSpec as P

step_size = 0.1
gravity = 1.0


def cross_rows(first, second):
    return jnp.stack(
        [
            first[1] * second[2] - first[2] * second[1],
            first[2] * second[0] - first[0] * second[2],
            first[0] * second[1] - first[1] * second[0],
        ]
    )


def raw_terms(points, wake_table):
    point_count = points.shape[1]
    wake_count = wake_table.shape[1]
    wake_width = math.gcd(wake_count, 2048)
    wake_place = wake_table[0:3]
    core_square = wake_table[3]
    tables = wake_table[4:10]
    place_blocks = wake_place.reshape(3, wake_count // wake_width, wake_width).transpose(1, 0, 2)
    table_blocks = tables.reshape(6, wake_count // wake_width, wake_width).transpose(1, 0, 2)
    core_blocks = core_square.reshape(wake_count // wake_width, wake_width)
    point_blocks = points.reshape(3, point_count // point_count, point_count).transpose(1, 0, 2)

    def one_block(point_group):

        def accumulate(running, parts):
            place_part, table_part, core_part = parts
            first_gap = point_group[0][:, None] - place_part[0][None, :]
            second_gap = point_group[1][:, None] - place_part[1][None, :]
            third_gap = point_group[2][:, None] - place_part[2][None, :]
            distance_sq = (
                first_gap * first_gap
                + second_gap * second_gap
                + third_gap * third_gap
                + core_part[None, :]
            )
            inverse_root = lax.rsqrt(distance_sq)
            kernel = inverse_root * inverse_root * inverse_root
            product = lax.dot_general(
                table_part, kernel, (((1,), (1,)), ((), ())), precision=lax.Precision.HIGH
            )
            return (running + product, None)

        total, _ = lax.scan(
            accumulate,
            jnp.zeros((6, point_count), jnp.float32),
            (place_blocks, table_blocks, core_blocks),
        )
        return total

    result = lax.map(one_block, point_blocks)
    return result.transpose(1, 0, 2).reshape(6, point_count)


def advance(arrived, raw_sums):
    points = arrived[0:3]
    velocity = arrived[3:6]
    live_flag = arrived[7]
    wind = (cross_rows(raw_sums[0:3], points) - raw_sums[3:6]) / (4.0 * math.pi)
    safe_tau = jnp.where(live_flag > 0.5, arrived[6], 1.0)
    rate = step_size / safe_tau
    upward = jnp.array([0.0, 0.0, 1.0], jnp.float32)[:, None]
    new_velocity = (velocity + rate[None, :] * wind - step_size * gravity * upward) / (
        1.0 + rate[None, :]
    )
    new_place = points + step_size * new_velocity
    return jnp.concatenate([new_place, new_velocity], axis=0) * live_flag[None, :]


def exact_place(values, placing):
    high = values.astype(jnp.bfloat16)
    rest = values - high.astype(jnp.float32)
    middle = rest.astype(jnp.bfloat16)
    low = (rest - middle.astype(jnp.float32)).astype(jnp.bfloat16)
    total = jnp.dot(high, placing, preferred_element_type=jnp.float32)
    total = total + jnp.dot(middle, placing, preferred_element_type=jnp.float32)
    return total + jnp.dot(low, placing, preferred_element_type=jnp.float32)


def prologue_kernel(
    count_ref, pos_ref, vel_ref, tau_ref, dest_ref, wpos_ref, wgam_ref, wcore_ref,
    out_ref, table_ref, *, regions, capacity,
):
    per_device = dest_ref.shape[0]
    slot_count = out_ref.shape[1]
    target = dest_ref[...]
    row = lax.broadcasted_iota(jnp.int32, (per_device, per_device), 0)
    col = lax.broadcasted_iota(jnp.int32, (per_device, per_device), 1)
    lower = (col < row).astype(jnp.bfloat16)
    region_id = lax.broadcasted_iota(jnp.int32, (per_device, regions), 1)
    onehot = (target == region_id).astype(jnp.float32)
    before = jnp.dot(lower, onehot.astype(jnp.bfloat16), preferred_element_type=jnp.float32)
    slot_rank = jnp.sum(before * onehot, axis=1, keepdims=True).astype(jnp.int32)
    column = target * capacity + slot_rank
    live = lax.broadcasted_iota(jnp.int32, (per_device, 1), 0) < count_ref[0]
    slot_id = lax.broadcasted_iota(jnp.int32, (per_device, slot_count), 1)
    placing = ((column == slot_id) & live).astype(jnp.bfloat16)
    out_ref[0:3, :] = exact_place(pos_ref[...], placing)
    out_ref[3:6, :] = exact_place(vel_ref[...], placing)
    out_ref[6:7, :] = exact_place(tau_ref[...], placing)
    ones = jnp.ones((1, per_device), jnp.bfloat16)
    out_ref[7:8, :] = jnp.dot(ones, placing, preferred_element_type=jnp.float32)
    place = [wpos_ref[i:i + 1, :] for i in range(3)]
    gamma = [wgam_ref[i:i + 1, :] for i in range(3)]
    core = wcore_ref[...]
    table_ref[0:3, :] = wpos_ref[...]
    table_ref[3:4, :] = core * core
    table_ref[4:7, :] = wgam_ref[...]
    table_ref[7:8, :] = gamma[1] * place[2] - gamma[2] * place[1]
    table_ref[8:9, :] = gamma[2] * place[0] - gamma[0] * place[2]
    table_ref[9:10, :] = gamma[0] * place[1] - gamma[1] * place[0]


def prologue(dust_pos, dust_vel, dust_tau, dest, counts, wake_pos, wake_gamma, wake_core):
    per_device = dust_tau.shape[0]
    regions = lax.axis_size("region")
    capacity = 2 * per_device // regions
    wake_count = wake_core.shape[0]
    vmem = pl.BlockSpec(memory_space=pltpu.VMEM)
    return pl.pallas_call(
        functools.partial(prologue_kernel, regions=regions, capacity=capacity),
        out_shape=(
            jax.ShapeDtypeStruct((8, regions * capacity), jnp.float32),
            jax.ShapeDtypeStruct((10, wake_count), jnp.float32),
        ),
        in_specs=[pl.BlockSpec(memory_space=pltpu.SMEM)] + [vmem] * 7,
        out_specs=(vmem, vmem),
    )(
        counts, dust_pos, dust_vel, dust_tau.reshape(1, per_device), dest,
        wake_pos, wake_gamma, wake_core.reshape(1, wake_count),
    )


def exchange_slots(outgoing, capacity):
    regions = lax.axis_size("region")
    if regions > 8:
        return lax.all_to_all(outgoing, "region", split_axis=1, concat_axis=1, tiled=True)
    region = lax.axis_index("region")
    blocks = outgoing.reshape(outgoing.shape[0], regions, capacity)
    by_shift = [jnp.take(blocks, region, axis=1)]
    for shift in range(1, regions):
        pairs = [(i, (i + shift) % regions) for i in range(regions)]
        sent = jnp.take(blocks, (region + shift) % regions, axis=1)
        by_shift.append(lax.ppermute(sent, "region", pairs))
    placed = []
    for source in range(regions):
        shift = (region - source) % regions
        block = by_shift[0]
        for other in range(1, regions):
            block = jnp.where(shift == other, by_shift[other], block)
        placed.append(block)
    return jnp.concatenate(placed, axis=1)


def body(dust_pos, dust_vel, dust_tau, dest, counts, wake_pos, wake_gamma, wake_core):
    per_device = dust_tau.shape[0]
    regions = lax.axis_size("region")
    capacity = 2 * per_device // regions
    outgoing, wake_table = prologue(
        dust_pos, dust_vel, dust_tau, dest, counts, wake_pos, wake_gamma, wake_core
    )
    outgoing, wake_table = lax.optimization_barrier((outgoing, wake_table))
    arrived = exchange_slots(outgoing, capacity)
    region_table = lax.all_gather(wake_table, "narrow", axis=1, tiled=True)
    points = arrived[0:3]
    raw_sums = raw_terms(points, region_table)
    return advance(arrived, raw_sums)


def solution(mesh):
    in_specs = (
        P(None, ("region", "narrow")),
        P(None, ("region", "narrow")),
        P(("region", "narrow")),
        P(("region", "narrow"), None),
        P(("region", "narrow")),
        P(None, ("region", "narrow")),
        P(None, ("region", "narrow")),
        P(("region", "narrow")),
    )
    out_specs = P(None, ("region", "narrow"))
    return jax.shard_map(body, mesh=mesh, in_specs=in_specs, out_specs=out_specs, check_vma=False)
```

```python
import functools
import math

import jax
import jax.numpy as jnp
from jax import lax
from jax.experimental import pallas as pl
from jax.experimental.pallas import tpu as pltpu
from jax.sharding import PartitionSpec as P

step_size = 0.1
gravity = 1.0


def cross_rows(first, second):
    return jnp.stack(
        [
            first[1] * second[2] - first[2] * second[1],
            first[2] * second[0] - first[0] * second[2],
            first[0] * second[1] - first[1] * second[0],
        ]
    )


def raw_terms(points, wake_table):
    point_count = points.shape[1]
    wake_count = wake_table.shape[1]
    wake_width = math.gcd(wake_count, 2048)
    wake_place = wake_table[0:3]
    core_square = wake_table[3]
    tables = wake_table[4:10]
    place_blocks = wake_place.reshape(3, wake_count // wake_width, wake_width).transpose(1, 0, 2)
    table_blocks = tables.reshape(6, wake_count // wake_width, wake_width).transpose(1, 0, 2)
    core_blocks = core_square.reshape(wake_count // wake_width, wake_width)
    point_blocks = points.reshape(3, point_count // point_count, point_count).transpose(1, 0, 2)

    def one_block(point_group):

        def accumulate(running, parts):
            place_part, table_part, core_part = parts
            first_gap = point_group[0][:, None] - place_part[0][None, :]
            second_gap = point_group[1][:, None] - place_part[1][None, :]
            third_gap = point_group[2][:, None] - place_part[2][None, :]
            distance_sq = (
                first_gap * first_gap
                + second_gap * second_gap
                + third_gap * third_gap
                + core_part[None, :]
            )
            inverse_root = lax.rsqrt(distance_sq)
            kernel = inverse_root * inverse_root * inverse_root
            product = lax.dot_general(
                table_part, kernel, (((1,), (1,)), ((), ())), precision=lax.Precision.HIGH
            )
            return (running + product, None)

        total, _ = lax.scan(
            accumulate,
            jnp.zeros((6, point_count), jnp.float32),
            (place_blocks, table_blocks, core_blocks),
        )
        return total

    result = lax.map(one_block, point_blocks)
    return result.transpose(1, 0, 2).reshape(6, point_count)


def advance(arrived, raw_sums):
    points = arrived[0:3]
    velocity = arrived[3:6]
    live_flag = arrived[7]
    wind = (cross_rows(raw_sums[0:3], points) - raw_sums[3:6]) / (4.0 * math.pi)
    safe_tau = jnp.where(live_flag > 0.5, arrived[6], 1.0)
    rate = step_size / safe_tau
    upward = jnp.array([0.0, 0.0, 1.0], jnp.float32)[:, None]
    new_velocity = (velocity + rate[None, :] * wind - step_size * gravity * upward) / (
        1.0 + rate[None, :]
    )
    new_place = points + step_size * new_velocity
    return jnp.concatenate([new_place, new_velocity], axis=0) * live_flag[None, :]


def exact_place(values, placing):
    high = values.astype(jnp.bfloat16)
    rest = values - high.astype(jnp.float32)
    middle = rest.astype(jnp.bfloat16)
    low = (rest - middle.astype(jnp.float32)).astype(jnp.bfloat16)
    contract = (((1,), (1,)), ((), ()))
    total = lax.dot_general(high, placing, contract, preferred_element_type=jnp.float32)
    total = total + lax.dot_general(middle, placing, contract, preferred_element_type=jnp.float32)
    return total + lax.dot_general(low, placing, contract, preferred_element_type=jnp.float32)


def prologue_kernel(
    count_ref, pos_ref, vel_ref, tau_ref, dest_ref, wpos_ref, wgam_ref, wcore_ref,
    out_ref, table_ref,
):
    regions, _, capacity = out_ref.shape
    per_device = dest_ref.shape[1]
    target = dest_ref[...]
    region_id = lax.broadcasted_iota(jnp.int32, (regions, per_device), 0)
    onehot = (target == region_id).astype(jnp.float32)
    row = lax.broadcasted_iota(jnp.int32, (per_device, per_device), 0)
    col = lax.broadcasted_iota(jnp.int32, (per_device, per_device), 1)
    upper = (row < col).astype(jnp.bfloat16)
    before = jnp.dot(onehot.astype(jnp.bfloat16), upper, preferred_element_type=jnp.float32)
    slot_rank = jnp.sum(before * onehot, axis=0, keepdims=True).astype(jnp.int32)
    column = target * capacity + slot_rank
    live = lax.broadcasted_iota(jnp.int32, (1, per_device), 1) < count_ref[0]
    pos = pos_ref[...]
    vel = vel_ref[...]
    tau = tau_ref[...]
    ones = jnp.ones((1, per_device), jnp.bfloat16)

    def one_region(d, carry):
        slot_id = lax.broadcasted_iota(jnp.int32, (capacity, per_device), 0) + d * capacity
        placing = ((column == slot_id) & live).astype(jnp.bfloat16)
        out_ref[d, 0:3, :] = exact_place(pos, placing)
        out_ref[d, 3:6, :] = exact_place(vel, placing)
        out_ref[d, 6:7, :] = exact_place(tau, placing)
        out_ref[d, 7:8, :] = lax.dot_general(
            ones, placing, (((1,), (1,)), ((), ())), preferred_element_type=jnp.float32
        )
        return carry

    lax.fori_loop(0, regions, one_region, 0)
    core = wcore_ref[...]
    table_ref[0:3, :] = wpos_ref[...]
    table_ref[3:4, :] = core * core
    table_ref[4:7, :] = wgam_ref[...]


def prologue(dust_pos, dust_vel, dust_tau, dest, counts, wake_pos, wake_gamma, wake_core):
    per_device = dust_tau.shape[0]
    regions = lax.axis_size("region")
    capacity = 2 * per_device // regions
    wake_count = wake_core.shape[0]
    vmem = pl.BlockSpec(memory_space=pltpu.VMEM)
    return pl.pallas_call(
        prologue_kernel,
        out_shape=(
            jax.ShapeDtypeStruct((regions, 8, capacity), jnp.float32),
            jax.ShapeDtypeStruct((7, wake_count), jnp.float32),
        ),
        in_specs=[pl.BlockSpec(memory_space=pltpu.SMEM)] + [vmem] * 7,
        out_specs=(vmem, vmem),
    )(
        counts, dust_pos, dust_vel, dust_tau.reshape(1, per_device), dest.reshape(1, per_device),
        wake_pos, wake_gamma, wake_core.reshape(1, wake_count),
    )


def exchange_slots(blocks):
    regions, rows, capacity = blocks.shape
    if regions > 8:
        arrived = lax.all_to_all(blocks, "region", split_axis=0, concat_axis=0, tiled=True)
        return arrived.transpose(1, 0, 2).reshape(rows, regions * capacity)
    region = lax.axis_index("region")
    by_shift = [blocks[region]]
    for shift in range(1, regions):
        pairs = [(i, (i + shift) % regions) for i in range(regions)]
        by_shift.append(lax.ppermute(blocks[(region + shift) % regions], "region", pairs))
    placed = []
    for source in range(regions):
        shift = (region - source) % regions
        block = by_shift[0]
        for other in range(1, regions):
            block = jnp.where(shift == other, by_shift[other], block)
        placed.append(block)
    return jnp.concatenate(placed, axis=1)


def wake_tables(gathered):
    place = gathered[0:3]
    gamma = gathered[4:7]
    return jnp.concatenate([gathered, cross_rows(gamma, place)], axis=0)


def body(dust_pos, dust_vel, dust_tau, dest, counts, wake_pos, wake_gamma, wake_core):
    outgoing, wake_table = prologue(
        dust_pos, dust_vel, dust_tau, dest, counts, wake_pos, wake_gamma, wake_core
    )
    outgoing, wake_table = lax.optimization_barrier((outgoing, wake_table))
    arrived = exchange_slots(outgoing)
    region_table = wake_tables(lax.all_gather(wake_table, "narrow", axis=1, tiled=True))
    points = arrived[0:3]
    raw_sums = raw_terms(points, region_table)
    return advance(arrived, raw_sums)


def solution(mesh):
    in_specs = (
        P(None, ("region", "narrow")),
        P(None, ("region", "narrow")),
        P(("region", "narrow")),
        P(("region", "narrow"), None),
        P(("region", "narrow")),
        P(None, ("region", "narrow")),
        P(None, ("region", "narrow")),
        P(("region", "narrow")),
    )
    out_specs = P(None, ("region", "narrow"))
    return jax.shard_map(body, mesh=mesh, in_specs=in_specs, out_specs=out_specs, check_vma=False)
```

```python
import functools
import math

import jax
import jax.numpy as jnp
from jax import lax
from jax.experimental import pallas as pl
from jax.experimental.pallas import tpu as pltpu
from jax.sharding import PartitionSpec as P

step_size = 0.1
gravity = 1.0


def cross_rows(first, second):
    return jnp.stack(
        [
            first[1] * second[2] - first[2] * second[1],
            first[2] * second[0] - first[0] * second[2],
            first[0] * second[1] - first[1] * second[0],
        ]
    )


def raw_terms(points, wake_table):
    point_count = points.shape[1]
    wake_count = wake_table.shape[1]
    wake_width = wake_count
    wake_place = wake_table[0:3]
    core_square = wake_table[3]
    tables = wake_table[4:10]
    place_blocks = wake_place.reshape(3, wake_count // wake_width, wake_width).transpose(1, 0, 2)
    table_blocks = tables.reshape(6, wake_count // wake_width, wake_width).transpose(1, 0, 2)
    core_blocks = core_square.reshape(wake_count // wake_width, wake_width)
    point_blocks = points.reshape(3, point_count // point_count, point_count).transpose(1, 0, 2)

    def one_block(point_group):

        def accumulate(running, parts):
            place_part, table_part, core_part = parts
            first_gap = point_group[0][:, None] - place_part[0][None, :]
            second_gap = point_group[1][:, None] - place_part[1][None, :]
            third_gap = point_group[2][:, None] - place_part[2][None, :]
            distance_sq = (
                first_gap * first_gap
                + second_gap * second_gap
                + third_gap * third_gap
                + core_part[None, :]
            )
            inverse_root = lax.rsqrt(distance_sq)
            kernel = inverse_root * inverse_root * inverse_root
            product = lax.dot_general(
                table_part, kernel, (((1,), (1,)), ((), ())), precision=lax.Precision.HIGH
            )
            return (running + product, None)

        total, _ = lax.scan(
            accumulate,
            jnp.zeros((6, point_count), jnp.float32),
            (place_blocks, table_blocks, core_blocks),
        )
        return total

    result = lax.map(one_block, point_blocks)
    return result.transpose(1, 0, 2).reshape(6, point_count)


def advance(arrived, raw_sums):
    points = arrived[0:3]
    velocity = arrived[3:6]
    live_flag = arrived[7]
    wind = (cross_rows(raw_sums[0:3], points) - raw_sums[3:6]) / (4.0 * math.pi)
    safe_tau = jnp.where(live_flag > 0.5, arrived[6], 1.0)
    rate = step_size / safe_tau
    upward = jnp.array([0.0, 0.0, 1.0], jnp.float32)[:, None]
    new_velocity = (velocity + rate[None, :] * wind - step_size * gravity * upward) / (
        1.0 + rate[None, :]
    )
    new_place = points + step_size * new_velocity
    return jnp.concatenate([new_place, new_velocity], axis=0) * live_flag[None, :]


def exact_place(values, placing):
    high = values.astype(jnp.bfloat16)
    rest = values - high.astype(jnp.float32)
    middle = rest.astype(jnp.bfloat16)
    low = (rest - middle.astype(jnp.float32)).astype(jnp.bfloat16)
    contract = (((1,), (1,)), ((), ()))
    total = lax.dot_general(high, placing, contract, preferred_element_type=jnp.float32)
    total = total + lax.dot_general(middle, placing, contract, preferred_element_type=jnp.float32)
    return total + lax.dot_general(low, placing, contract, preferred_element_type=jnp.float32)


def prologue_kernel(
    count_ref, pos_ref, vel_ref, tau_ref, dest_ref, wpos_ref, wgam_ref, wcore_ref,
    out_ref, table_ref,
):
    regions, _, capacity = out_ref.shape
    per_device = dest_ref.shape[1]
    target = dest_ref[...]
    region_id = lax.broadcasted_iota(jnp.int32, (regions, per_device), 0)
    onehot = (target == region_id).astype(jnp.float32)
    row = lax.broadcasted_iota(jnp.int32, (per_device, per_device), 0)
    col = lax.broadcasted_iota(jnp.int32, (per_device, per_device), 1)
    upper = (row < col).astype(jnp.bfloat16)
    before = jnp.dot(onehot.astype(jnp.bfloat16), upper, preferred_element_type=jnp.float32)
    slot_rank = jnp.sum(before * onehot, axis=0, keepdims=True).astype(jnp.int32)
    column = target * capacity + slot_rank
    live = lax.broadcasted_iota(jnp.int32, (1, per_device), 1) < count_ref[0]
    pos = pos_ref[...]
    vel = vel_ref[...]
    tau = tau_ref[...]
    ones = jnp.ones((1, per_device), jnp.bfloat16)

    def one_region(d, carry):
        slot_id = lax.broadcasted_iota(jnp.int32, (capacity, per_device), 0) + d * capacity
        placing = ((column == slot_id) & live).astype(jnp.bfloat16)
        out_ref[d, 0:3, :] = exact_place(pos, placing)
        out_ref[d, 3:6, :] = exact_place(vel, placing)
        out_ref[d, 6:7, :] = exact_place(tau, placing)
        out_ref[d, 7:8, :] = lax.dot_general(
            ones, placing, (((1,), (1,)), ((), ())), preferred_element_type=jnp.float32
        )
        return carry

    lax.fori_loop(0, regions, one_region, 0)
    core = wcore_ref[...]
    table_ref[0:3, :] = wpos_ref[...]
    table_ref[3:4, :] = core * core
    table_ref[4:7, :] = wgam_ref[...]


def prologue(dust_pos, dust_vel, dust_tau, dest, counts, wake_pos, wake_gamma, wake_core):
    per_device = dust_tau.shape[0]
    regions = lax.axis_size("region")
    capacity = 2 * per_device // regions
    wake_count = wake_core.shape[0]
    vmem = pl.BlockSpec(memory_space=pltpu.VMEM)
    return pl.pallas_call(
        prologue_kernel,
        out_shape=(
            jax.ShapeDtypeStruct((regions, 8, capacity), jnp.float32),
            jax.ShapeDtypeStruct((7, wake_count), jnp.float32),
        ),
        in_specs=[pl.BlockSpec(memory_space=pltpu.SMEM)] + [vmem] * 7,
        out_specs=(vmem, vmem),
    )(
        counts, dust_pos, dust_vel, dust_tau.reshape(1, per_device), dest.reshape(1, per_device),
        wake_pos, wake_gamma, wake_core.reshape(1, wake_count),
    )


def exchange_slots(blocks):
    regions, rows, capacity = blocks.shape
    if regions > 8:
        arrived = lax.all_to_all(blocks, "region", split_axis=0, concat_axis=0, tiled=True)
        return arrived.transpose(1, 0, 2).reshape(rows, regions * capacity)
    region = lax.axis_index("region")
    by_shift = [blocks[region]]
    for shift in range(1, regions):
        pairs = [(i, (i + shift) % regions) for i in range(regions)]
        by_shift.append(lax.ppermute(blocks[(region + shift) % regions], "region", pairs))
    placed = []
    for source in range(regions):
        shift = (region - source) % regions
        block = by_shift[0]
        for other in range(1, regions):
            block = jnp.where(shift == other, by_shift[other], block)
        placed.append(block)
    return jnp.concatenate(placed, axis=1)


def wake_tables(gathered):
    place = gathered[0:3]
    gamma = gathered[4:7]
    return jnp.concatenate([gathered, cross_rows(gamma, place)], axis=0)


def body(dust_pos, dust_vel, dust_tau, dest, counts, wake_pos, wake_gamma, wake_core):
    outgoing, wake_table = prologue(
        dust_pos, dust_vel, dust_tau, dest, counts, wake_pos, wake_gamma, wake_core
    )
    outgoing, wake_table = lax.optimization_barrier((outgoing, wake_table))
    arrived = exchange_slots(outgoing)
    region_table = wake_tables(lax.all_gather(wake_table, "narrow", axis=1, tiled=True))
    points = arrived[0:3]
    raw_sums = raw_terms(points, region_table)
    return advance(arrived, raw_sums)


def solution(mesh):
    in_specs = (
        P(None, ("region", "narrow")),
        P(None, ("region", "narrow")),
        P(("region", "narrow")),
        P(("region", "narrow"), None),
        P(("region", "narrow")),
        P(None, ("region", "narrow")),
        P(None, ("region", "narrow")),
        P(("region", "narrow")),
    )
    out_specs = P(None, ("region", "narrow"))
    return jax.shard_map(body, mesh=mesh, in_specs=in_specs, out_specs=out_specs, check_vma=False)
```

```python
import functools
import math

import jax
import jax.numpy as jnp
from jax import lax
from jax.experimental import pallas as pl
from jax.experimental.pallas import tpu as pltpu
from jax.sharding import PartitionSpec as P

step_size = 0.1
gravity = 1.0


def cross_rows(first, second):
    return jnp.stack(
        [
            first[1] * second[2] - first[2] * second[1],
            first[2] * second[0] - first[0] * second[2],
            first[0] * second[1] - first[1] * second[0],
        ]
    )


def raw_terms(points, wake_table):
    point_count = points.shape[1]
    wake_count = wake_table.shape[1]
    wake_width = math.gcd(wake_count, 2048)
    wake_place = wake_table[0:3]
    core_square = wake_table[3]
    tables = wake_table[4:10]
    place_blocks = wake_place.reshape(3, wake_count // wake_width, wake_width).transpose(1, 0, 2)
    table_blocks = tables.reshape(6, wake_count // wake_width, wake_width).transpose(1, 0, 2)
    core_blocks = core_square.reshape(wake_count // wake_width, wake_width)
    point_blocks = points.reshape(3, point_count // point_count, point_count).transpose(1, 0, 2)

    def one_block(point_group):

        def accumulate(running, parts):
            place_part, table_part, core_part = parts
            first_gap = point_group[0][:, None] - place_part[0][None, :]
            second_gap = point_group[1][:, None] - place_part[1][None, :]
            third_gap = point_group[2][:, None] - place_part[2][None, :]
            distance_sq = (
                first_gap * first_gap
                + second_gap * second_gap
                + third_gap * third_gap
                + core_part[None, :]
            )
            inverse_root = lax.rsqrt(distance_sq)
            kernel = inverse_root * inverse_root * inverse_root
            product = lax.dot_general(
                table_part, kernel, (((1,), (1,)), ((), ())), precision=lax.Precision.HIGH
            )
            return (running + product, None)

        total, _ = lax.scan(
            accumulate,
            jnp.zeros((6, point_count), jnp.float32),
            (place_blocks, table_blocks, core_blocks),
        )
        return total

    result = lax.map(one_block, point_blocks)
    return result.transpose(1, 0, 2).reshape(6, point_count)


def advance(arrived, raw_sums):
    points = arrived[0:3]
    velocity = arrived[3:6]
    live_flag = arrived[7]
    wind = (cross_rows(raw_sums[0:3], points) - raw_sums[3:6]) / (4.0 * math.pi)
    safe_tau = jnp.where(live_flag > 0.5, arrived[6], 1.0)
    rate = step_size / safe_tau
    upward = jnp.array([0.0, 0.0, 1.0], jnp.float32)[:, None]
    new_velocity = (velocity + rate[None, :] * wind - step_size * gravity * upward) / (
        1.0 + rate[None, :]
    )
    new_place = points + step_size * new_velocity
    return jnp.concatenate([new_place, new_velocity], axis=0) * live_flag[None, :]


def exact_place(values, placing):
    high = values.astype(jnp.bfloat16)
    rest = values - high.astype(jnp.float32)
    middle = rest.astype(jnp.bfloat16)
    low = (rest - middle.astype(jnp.float32)).astype(jnp.bfloat16)
    contract = (((1,), (1,)), ((), ()))
    total = lax.dot_general(high, placing, contract, preferred_element_type=jnp.float32)
    total = total + lax.dot_general(middle, placing, contract, preferred_element_type=jnp.float32)
    return total + lax.dot_general(low, placing, contract, preferred_element_type=jnp.float32)


def prologue_kernel(
    count_ref, pos_ref, vel_ref, tau_ref, dest_ref, wpos_ref, wgam_ref, wcore_ref,
    out_ref, table_ref, state_ref,
):
    regions, _, capacity = out_ref.shape
    per_device = dest_ref.shape[1]
    target = dest_ref[...]
    region_id = lax.broadcasted_iota(jnp.int32, (regions, per_device), 0)
    onehot = (target == region_id).astype(jnp.float32)
    row = lax.broadcasted_iota(jnp.int32, (per_device, per_device), 0)
    col = lax.broadcasted_iota(jnp.int32, (per_device, per_device), 1)
    upper = (row < col).astype(jnp.bfloat16)
    before = jnp.dot(onehot.astype(jnp.bfloat16), upper, preferred_element_type=jnp.float32)
    slot_rank = jnp.sum(before * onehot, axis=0, keepdims=True).astype(jnp.int32)
    column = target * capacity + slot_rank
    live = lax.broadcasted_iota(jnp.int32, (1, per_device), 1) < count_ref[0]
    state_ref[0:3, :] = pos_ref[...]
    state_ref[3:6, :] = vel_ref[...]
    state_ref[6:7, :] = tau_ref[...]
    state_ref[7:8, :] = jnp.ones((1, per_device), jnp.float32)
    state = state_ref[...]
    region = lax.axis_index("region")

    def one_shift(shift, carry):
        dest_region = (region + shift) % regions
        slot_id = lax.broadcasted_iota(jnp.int32, (capacity, per_device), 0) + dest_region * capacity
        placing = ((column == slot_id) & live).astype(jnp.bfloat16)
        out_ref[shift] = exact_place(state, placing)
        return carry

    lax.fori_loop(0, regions, one_shift, 0)
    core = wcore_ref[...]
    table_ref[0:3, :] = wpos_ref[...]
    table_ref[3:4, :] = core * core
    table_ref[4:7, :] = wgam_ref[...]


def prologue(dust_pos, dust_vel, dust_tau, dest, counts, wake_pos, wake_gamma, wake_core):
    per_device = dust_tau.shape[0]
    regions = lax.axis_size("region")
    capacity = 2 * per_device // regions
    wake_count = wake_core.shape[0]
    vmem = pl.BlockSpec(memory_space=pltpu.VMEM)
    return pl.pallas_call(
        prologue_kernel,
        out_shape=(
            jax.ShapeDtypeStruct((regions, 8, capacity), jnp.float32),
            jax.ShapeDtypeStruct((7, wake_count), jnp.float32),
        ),
        in_specs=[pl.BlockSpec(memory_space=pltpu.SMEM)] + [vmem] * 7,
        out_specs=(vmem, vmem),
        scratch_shapes=[pltpu.VMEM((8, per_device), jnp.float32)],
    )(
        counts, dust_pos, dust_vel, dust_tau.reshape(1, per_device), dest.reshape(1, per_device),
        wake_pos, wake_gamma, wake_core.reshape(1, wake_count),
    )


def exchange_slots(by_offset):
    regions, rows, capacity = by_offset.shape
    region = lax.axis_index("region")
    if regions > 8:
        back = (jnp.arange(regions, dtype=jnp.int32) - region) % regions
        blocks = jnp.take(by_offset, back, axis=0)
        arrived = lax.all_to_all(blocks, "region", split_axis=0, concat_axis=0, tiled=True)
        return arrived.transpose(1, 0, 2).reshape(rows, regions * capacity)
    by_shift = [by_offset[0]]
    for shift in range(1, regions):
        pairs = [(i, (i + shift) % regions) for i in range(regions)]
        by_shift.append(lax.ppermute(by_offset[shift], "region", pairs))
    placed = []
    for source in range(regions):
        shift = (region - source) % regions
        block = by_shift[0]
        for other in range(1, regions):
            block = jnp.where(shift == other, by_shift[other], block)
        placed.append(block)
    return jnp.concatenate(placed, axis=1)


def wake_tables(gathered):
    place = gathered[0:3]
    gamma = gathered[4:7]
    return jnp.concatenate([gathered, cross_rows(gamma, place)], axis=0)


def body(dust_pos, dust_vel, dust_tau, dest, counts, wake_pos, wake_gamma, wake_core):
    outgoing, wake_table = prologue(
        dust_pos, dust_vel, dust_tau, dest, counts, wake_pos, wake_gamma, wake_core
    )
    outgoing, wake_table = lax.optimization_barrier((outgoing, wake_table))
    arrived = exchange_slots(outgoing)
    region_table = wake_tables(lax.all_gather(wake_table, "narrow", axis=1, tiled=True))
    points = arrived[0:3]
    raw_sums = raw_terms(points, region_table)
    return advance(arrived, raw_sums)


def solution(mesh):
    in_specs = (
        P(None, ("region", "narrow")),
        P(None, ("region", "narrow")),
        P(("region", "narrow")),
        P(("region", "narrow"), None),
        P(("region", "narrow")),
        P(None, ("region", "narrow")),
        P(None, ("region", "narrow")),
        P(("region", "narrow")),
    )
    out_specs = P(None, ("region", "narrow"))
    return jax.shard_map(body, mesh=mesh, in_specs=in_specs, out_specs=out_specs, check_vma=False)
```

```python
import functools
import math

import jax
import jax.numpy as jnp
from jax import lax
from jax.experimental import pallas as pl
from jax.experimental.pallas import tpu as pltpu
from jax.sharding import PartitionSpec as P

step_size = 0.1
gravity = 1.0


def cross_rows(first, second):
    return jnp.stack(
        [
            first[1] * second[2] - first[2] * second[1],
            first[2] * second[0] - first[0] * second[2],
            first[0] * second[1] - first[1] * second[0],
        ]
    )


def raw_terms(points, wake_table):
    point_count = points.shape[1]
    wake_count = wake_table.shape[1]
    wake_width = math.gcd(wake_count, 2048)
    wake_place = wake_table[0:3]
    core_square = wake_table[3]
    tables = wake_table[4:10]
    place_blocks = wake_place.reshape(3, wake_count // wake_width, wake_width).transpose(1, 0, 2)
    table_blocks = tables.reshape(6, wake_count // wake_width, wake_width).transpose(1, 0, 2)
    core_blocks = core_square.reshape(wake_count // wake_width, wake_width)
    point_blocks = points.reshape(3, point_count // point_count, point_count).transpose(1, 0, 2)

    def one_block(point_group):

        def accumulate(running, parts):
            place_part, table_part, core_part = parts
            first_gap = point_group[0][:, None] - place_part[0][None, :]
            second_gap = point_group[1][:, None] - place_part[1][None, :]
            third_gap = point_group[2][:, None] - place_part[2][None, :]
            distance_sq = (
                first_gap * first_gap
                + second_gap * second_gap
                + third_gap * third_gap
                + core_part[None, :]
            )
            inverse_root = lax.rsqrt(distance_sq)
            kernel = inverse_root * inverse_root * inverse_root
            product = lax.dot_general(
                table_part, kernel, (((1,), (1,)), ((), ())), precision=lax.Precision.HIGH
            )
            return (running + product, None)

        total, _ = lax.scan(
            accumulate,
            jnp.zeros((6, point_count), jnp.float32),
            (place_blocks, table_blocks, core_blocks),
        )
        return total

    result = lax.map(one_block, point_blocks)
    return result.transpose(1, 0, 2).reshape(6, point_count)


def advance(arrived, raw_sums):
    points = arrived[0:3]
    velocity = arrived[3:6]
    live_flag = arrived[7]
    wind = (cross_rows(raw_sums[0:3], points) - raw_sums[3:6]) / (4.0 * math.pi)
    safe_tau = jnp.where(live_flag > 0.5, arrived[6], 1.0)
    rate = step_size / safe_tau
    upward = jnp.array([0.0, 0.0, 1.0], jnp.float32)[:, None]
    new_velocity = (velocity + rate[None, :] * wind - step_size * gravity * upward) / (
        1.0 + rate[None, :]
    )
    new_place = points + step_size * new_velocity
    return jnp.concatenate([new_place, new_velocity], axis=0) * live_flag[None, :]


def exact_place(values, placing):
    high = values.astype(jnp.bfloat16)
    rest = values - high.astype(jnp.float32)
    middle = rest.astype(jnp.bfloat16)
    low = (rest - middle.astype(jnp.float32)).astype(jnp.bfloat16)
    contract = (((1,), (1,)), ((), ()))
    total = lax.dot_general(high, placing, contract, preferred_element_type=jnp.float32)
    total = total + lax.dot_general(middle, placing, contract, preferred_element_type=jnp.float32)
    return total + lax.dot_general(low, placing, contract, preferred_element_type=jnp.float32)


def prologue_kernel(
    count_ref, pos_ref, vel_ref, tau_ref, dest_ref, wpos_ref, wgam_ref, wcore_ref, *refs
):
    out_refs = refs[:-2]
    table_ref, state_ref = refs[-2:]
    regions = len(out_refs)
    capacity = out_refs[0].shape[1]
    per_device = dest_ref.shape[1]
    target = dest_ref[...]
    region_id = lax.broadcasted_iota(jnp.int32, (regions, per_device), 0)
    onehot = (target == region_id).astype(jnp.float32)
    row = lax.broadcasted_iota(jnp.int32, (per_device, per_device), 0)
    col = lax.broadcasted_iota(jnp.int32, (per_device, per_device), 1)
    upper = (row < col).astype(jnp.bfloat16)
    before = jnp.dot(onehot.astype(jnp.bfloat16), upper, preferred_element_type=jnp.float32)
    slot_rank = jnp.sum(before * onehot, axis=0, keepdims=True).astype(jnp.int32)
    column = target * capacity + slot_rank
    live = lax.broadcasted_iota(jnp.int32, (1, per_device), 1) < count_ref[0]
    state_ref[0:3, :] = pos_ref[...]
    state_ref[3:6, :] = vel_ref[...]
    state_ref[6:7, :] = tau_ref[...]
    state_ref[7:8, :] = jnp.ones((1, per_device), jnp.float32)
    state = state_ref[...]
    region = lax.axis_index("region")

    for shift, out_ref in enumerate(out_refs):
        dest_region = (region + shift) % regions
        slot_id = lax.broadcasted_iota(jnp.int32, (capacity, per_device), 0) + dest_region * capacity
        placing = ((column == slot_id) & live).astype(jnp.bfloat16)
        out_ref[...] = exact_place(state, placing)
    core = wcore_ref[...]
    table_ref[0:3, :] = wpos_ref[...]
    table_ref[3:4, :] = core * core
    table_ref[4:7, :] = wgam_ref[...]


def prologue(dust_pos, dust_vel, dust_tau, dest, counts, wake_pos, wake_gamma, wake_core):
    per_device = dust_tau.shape[0]
    regions = lax.axis_size("region")
    capacity = 2 * per_device // regions
    wake_count = wake_core.shape[0]
    vmem = pl.BlockSpec(memory_space=pltpu.VMEM)
    return pl.pallas_call(
        prologue_kernel,
        out_shape=tuple(
            [jax.ShapeDtypeStruct((8, capacity), jnp.float32)] * regions
            + [jax.ShapeDtypeStruct((7, wake_count), jnp.float32)]
        ),
        in_specs=[pl.BlockSpec(memory_space=pltpu.SMEM)] + [vmem] * 7,
        out_specs=tuple([vmem] * (regions + 1)),
        scratch_shapes=[pltpu.VMEM((8, per_device), jnp.float32)],
    )(
        counts, dust_pos, dust_vel, dust_tau.reshape(1, per_device), dest.reshape(1, per_device),
        wake_pos, wake_gamma, wake_core.reshape(1, wake_count),
    )


def exchange_slots(by_offset):
    regions = len(by_offset)
    rows, capacity = by_offset[0].shape
    region = lax.axis_index("region")
    if regions > 8:
        by_offset = jnp.stack(by_offset)
        back = (jnp.arange(regions, dtype=jnp.int32) - region) % regions
        blocks = jnp.take(by_offset, back, axis=0)
        arrived = lax.all_to_all(blocks, "region", split_axis=0, concat_axis=0, tiled=True)
        return arrived.transpose(1, 0, 2).reshape(rows, regions * capacity)
    by_shift = [by_offset[0]]
    for shift in range(1, regions):
        pairs = [(i, (i + shift) % regions) for i in range(regions)]
        by_shift.append(lax.ppermute(by_offset[shift], "region", pairs))
    placed = []
    for source in range(regions):
        shift = (region - source) % regions
        block = by_shift[0]
        for other in range(1, regions):
            block = jnp.where(shift == other, by_shift[other], block)
        placed.append(block)
    return jnp.concatenate(placed, axis=1)


def wake_tables(gathered):
    place = gathered[0:3]
    gamma = gathered[4:7]
    return jnp.concatenate([gathered, cross_rows(gamma, place)], axis=0)


def body(dust_pos, dust_vel, dust_tau, dest, counts, wake_pos, wake_gamma, wake_core):
    *outgoing, wake_table = prologue(
        dust_pos, dust_vel, dust_tau, dest, counts, wake_pos, wake_gamma, wake_core
    )
    outgoing, wake_table = lax.optimization_barrier((tuple(outgoing), wake_table))
    arrived = exchange_slots(outgoing)
    region_table = wake_tables(lax.all_gather(wake_table, "narrow", axis=1, tiled=True))
    points = arrived[0:3]
    raw_sums = raw_terms(points, region_table)
    return advance(arrived, raw_sums)


def solution(mesh):
    in_specs = (
        P(None, ("region", "narrow")),
        P(None, ("region", "narrow")),
        P(("region", "narrow")),
        P(("region", "narrow"), None),
        P(("region", "narrow")),
        P(None, ("region", "narrow")),
        P(None, ("region", "narrow")),
        P(("region", "narrow")),
    )
    out_specs = P(None, ("region", "narrow"))
    return jax.shard_map(body, mesh=mesh, in_specs=in_specs, out_specs=out_specs, check_vma=False)
```

```python
import functools
import math

import jax
import jax.numpy as jnp
from jax import lax
from jax.experimental import pallas as pl
from jax.experimental.pallas import tpu as pltpu
from jax.sharding import PartitionSpec as P

step_size = 0.1
gravity = 1.0


def cross_rows(first, second):
    return jnp.stack(
        [
            first[1] * second[2] - first[2] * second[1],
            first[2] * second[0] - first[0] * second[2],
            first[0] * second[1] - first[1] * second[0],
        ]
    )


def raw_terms(points, wake_table):
    point_count = points.shape[1]
    wake_count = wake_table.shape[1]
    wake_width = math.gcd(wake_count, 2048)
    wake_place = wake_table[0:3]
    core_square = wake_table[3]
    tables = wake_table[4:10]
    place_blocks = wake_place.reshape(3, wake_count // wake_width, wake_width).transpose(1, 0, 2)
    table_blocks = tables.reshape(6, wake_count // wake_width, wake_width).transpose(1, 0, 2)
    core_blocks = core_square.reshape(wake_count // wake_width, wake_width)
    point_blocks = points.reshape(3, point_count // point_count, point_count).transpose(1, 0, 2)

    def one_block(point_group):

        def accumulate(running, parts):
            place_part, table_part, core_part = parts
            first_gap = point_group[0][:, None] - place_part[0][None, :]
            second_gap = point_group[1][:, None] - place_part[1][None, :]
            third_gap = point_group[2][:, None] - place_part[2][None, :]
            distance_sq = (
                first_gap * first_gap
                + second_gap * second_gap
                + third_gap * third_gap
                + core_part[None, :]
            )
            inverse_root = lax.rsqrt(distance_sq)
            kernel = inverse_root * inverse_root * inverse_root
            product = lax.dot_general(
                kernel, table_part, (((1,), (1,)), ((), ())), precision=lax.Precision.HIGH
            )
            return (running + product, None)

        total, _ = lax.scan(
            accumulate,
            jnp.zeros((point_count, 6), jnp.float32),
            (place_blocks, table_blocks, core_blocks),
        )
        return total.T

    result = lax.map(one_block, point_blocks)
    return result.transpose(1, 0, 2).reshape(6, point_count)


def advance(arrived, raw_sums):
    points = arrived[0:3]
    velocity = arrived[3:6]
    live_flag = arrived[7]
    wind = (cross_rows(raw_sums[0:3], points) - raw_sums[3:6]) / (4.0 * math.pi)
    safe_tau = jnp.where(live_flag > 0.5, arrived[6], 1.0)
    rate = step_size / safe_tau
    upward = jnp.array([0.0, 0.0, 1.0], jnp.float32)[:, None]
    new_velocity = (velocity + rate[None, :] * wind - step_size * gravity * upward) / (
        1.0 + rate[None, :]
    )
    new_place = points + step_size * new_velocity
    return jnp.concatenate([new_place, new_velocity], axis=0) * live_flag[None, :]


def exact_place(values, placing):
    high = values.astype(jnp.bfloat16)
    rest = values - high.astype(jnp.float32)
    middle = rest.astype(jnp.bfloat16)
    low = (rest - middle.astype(jnp.float32)).astype(jnp.bfloat16)
    contract = (((1,), (1,)), ((), ()))
    total = lax.dot_general(high, placing, contract, preferred_element_type=jnp.float32)
    total = total + lax.dot_general(middle, placing, contract, preferred_element_type=jnp.float32)
    return total + lax.dot_general(low, placing, contract, preferred_element_type=jnp.float32)


def prologue_kernel(
    count_ref, pos_ref, vel_ref, tau_ref, dest_ref, wpos_ref, wgam_ref, wcore_ref, *refs
):
    out_refs = refs[:-2]
    table_ref, state_ref = refs[-2:]
    regions = len(out_refs)
    capacity = out_refs[0].shape[1]
    per_device = dest_ref.shape[1]
    target = dest_ref[...]
    region_id = lax.broadcasted_iota(jnp.int32, (regions, per_device), 0)
    onehot = (target == region_id).astype(jnp.float32)
    row = lax.broadcasted_iota(jnp.int32, (per_device, per_device), 0)
    col = lax.broadcasted_iota(jnp.int32, (per_device, per_device), 1)
    upper = (row < col).astype(jnp.bfloat16)
    before = jnp.dot(onehot.astype(jnp.bfloat16), upper, preferred_element_type=jnp.float32)
    slot_rank = jnp.sum(before * onehot, axis=0, keepdims=True).astype(jnp.int32)
    column = target * capacity + slot_rank
    live = lax.broadcasted_iota(jnp.int32, (1, per_device), 1) < count_ref[0]
    state_ref[0:3, :] = pos_ref[...]
    state_ref[3:6, :] = vel_ref[...]
    state_ref[6:7, :] = tau_ref[...]
    state_ref[7:8, :] = jnp.ones((1, per_device), jnp.float32)
    state = state_ref[...]
    region = lax.axis_index("region")

    for shift, out_ref in enumerate(out_refs):
        dest_region = (region + shift) % regions
        slot_id = lax.broadcasted_iota(jnp.int32, (capacity, per_device), 0) + dest_region * capacity
        placing = ((column == slot_id) & live).astype(jnp.bfloat16)
        out_ref[...] = exact_place(state, placing)
    core = wcore_ref[...]
    table_ref[0:3, :] = wpos_ref[...]
    table_ref[3:4, :] = core * core
    table_ref[4:7, :] = wgam_ref[...]


def prologue(dust_pos, dust_vel, dust_tau, dest, counts, wake_pos, wake_gamma, wake_core):
    per_device = dust_tau.shape[0]
    regions = lax.axis_size("region")
    capacity = 2 * per_device // regions
    wake_count = wake_core.shape[0]
    vmem = pl.BlockSpec(memory_space=pltpu.VMEM)
    return pl.pallas_call(
        prologue_kernel,
        out_shape=tuple(
            [jax.ShapeDtypeStruct((8, capacity), jnp.float32)] * regions
            + [jax.ShapeDtypeStruct((7, wake_count), jnp.float32)]
        ),
        in_specs=[pl.BlockSpec(memory_space=pltpu.SMEM)] + [vmem] * 7,
        out_specs=tuple([vmem] * (regions + 1)),
        scratch_shapes=[pltpu.VMEM((8, per_device), jnp.float32)],
    )(
        counts, dust_pos, dust_vel, dust_tau.reshape(1, per_device), dest.reshape(1, per_device),
        wake_pos, wake_gamma, wake_core.reshape(1, wake_count),
    )


def exchange_slots(by_offset):
    regions = len(by_offset)
    rows, capacity = by_offset[0].shape
    region = lax.axis_index("region")
    if regions > 8:
        by_offset = jnp.stack(by_offset)
        back = (jnp.arange(regions, dtype=jnp.int32) - region) % regions
        blocks = jnp.take(by_offset, back, axis=0)
        arrived = lax.all_to_all(blocks, "region", split_axis=0, concat_axis=0, tiled=True)
        return arrived.transpose(1, 0, 2).reshape(rows, regions * capacity)
    by_shift = [by_offset[0]]
    for shift in range(1, regions):
        pairs = [(i, (i + shift) % regions) for i in range(regions)]
        by_shift.append(lax.ppermute(by_offset[shift], "region", pairs))
    placed = []
    for source in range(regions):
        shift = (region - source) % regions
        block = by_shift[0]
        for other in range(1, regions):
            block = jnp.where(shift == other, by_shift[other], block)
        placed.append(block)
    return jnp.concatenate(placed, axis=1)


def wake_tables(gathered):
    place = gathered[0:3]
    gamma = gathered[4:7]
    return jnp.concatenate([gathered, cross_rows(gamma, place)], axis=0)


def body(dust_pos, dust_vel, dust_tau, dest, counts, wake_pos, wake_gamma, wake_core):
    *outgoing, wake_table = prologue(
        dust_pos, dust_vel, dust_tau, dest, counts, wake_pos, wake_gamma, wake_core
    )
    outgoing, wake_table = lax.optimization_barrier((tuple(outgoing), wake_table))
    arrived = exchange_slots(outgoing)
    region_table = wake_tables(lax.all_gather(wake_table, "narrow", axis=1, tiled=True))
    points = arrived[0:3]
    raw_sums = raw_terms(points, region_table)
    return advance(arrived, raw_sums)


def solution(mesh):
    in_specs = (
        P(None, ("region", "narrow")),
        P(None, ("region", "narrow")),
        P(("region", "narrow")),
        P(("region", "narrow"), None),
        P(("region", "narrow")),
        P(None, ("region", "narrow")),
        P(None, ("region", "narrow")),
        P(("region", "narrow")),
    )
    out_specs = P(None, ("region", "narrow"))
    return jax.shard_map(body, mesh=mesh, in_specs=in_specs, out_specs=out_specs, check_vma=False)
```

```python
import functools
import math

import jax
import jax.numpy as jnp
from jax import lax
from jax.experimental import pallas as pl
from jax.experimental.pallas import tpu as pltpu
from jax.sharding import PartitionSpec as P

step_size = 0.1
gravity = 1.0


def cross_rows(first, second):
    return jnp.stack(
        [
            first[1] * second[2] - first[2] * second[1],
            first[2] * second[0] - first[0] * second[2],
            first[0] * second[1] - first[1] * second[0],
        ]
    )


def raw_terms(points, wake_table):
    point_count = points.shape[1]
    wake_count = wake_table.shape[1]
    wake_width = math.gcd(wake_count, 2048)
    wake_place = wake_table[0:3]
    core_square = wake_table[3]
    tables = wake_table[4:10]
    wake_offset = (
        wake_place[0] * wake_place[0]
        + wake_place[1] * wake_place[1]
        + wake_place[2] * wake_place[2]
        + core_square
    )
    place_blocks = (-2.0 * wake_place).reshape(3, wake_count // wake_width, wake_width).transpose(1, 0, 2)
    table_blocks = tables.reshape(6, wake_count // wake_width, wake_width).transpose(1, 0, 2)
    core_blocks = wake_offset.reshape(wake_count // wake_width, wake_width)
    point_blocks = points.reshape(3, point_count // point_count, point_count).transpose(1, 0, 2)

    def one_block(point_group):
        point_sq = (
            point_group[0] * point_group[0]
            + point_group[1] * point_group[1]
            + point_group[2] * point_group[2]
        )

        def accumulate(running, parts):
            scaled_place, table_part, offset_part = parts
            distance_sq = (
                (point_sq[:, None] + offset_part[None, :])
                + point_group[0][:, None] * scaled_place[0][None, :]
                + point_group[1][:, None] * scaled_place[1][None, :]
                + point_group[2][:, None] * scaled_place[2][None, :]
            )
            inverse_root = lax.rsqrt(distance_sq)
            kernel = inverse_root * inverse_root * inverse_root
            product = lax.dot_general(
                table_part, kernel, (((1,), (1,)), ((), ())), precision=lax.Precision.HIGH
            )
            return (running + product, None)

        total, _ = lax.scan(
            accumulate,
            jnp.zeros((6, point_count), jnp.float32),
            (place_blocks, table_blocks, core_blocks),
        )
        return total

    result = lax.map(one_block, point_blocks)
    return result.transpose(1, 0, 2).reshape(6, point_count)


def advance(arrived, raw_sums):
    points = arrived[0:3]
    velocity = arrived[3:6]
    live_flag = arrived[7]
    wind = (cross_rows(raw_sums[0:3], points) - raw_sums[3:6]) / (4.0 * math.pi)
    safe_tau = jnp.where(live_flag > 0.5, arrived[6], 1.0)
    rate = step_size / safe_tau
    upward = jnp.array([0.0, 0.0, 1.0], jnp.float32)[:, None]
    new_velocity = (velocity + rate[None, :] * wind - step_size * gravity * upward) / (
        1.0 + rate[None, :]
    )
    new_place = points + step_size * new_velocity
    return jnp.concatenate([new_place, new_velocity], axis=0) * live_flag[None, :]


def exact_place(values, placing):
    high = values.astype(jnp.bfloat16)
    rest = values - high.astype(jnp.float32)
    middle = rest.astype(jnp.bfloat16)
    low = (rest - middle.astype(jnp.float32)).astype(jnp.bfloat16)
    contract = (((1,), (1,)), ((), ()))
    total = lax.dot_general(high, placing, contract, preferred_element_type=jnp.float32)
    total = total + lax.dot_general(middle, placing, contract, preferred_element_type=jnp.float32)
    return total + lax.dot_general(low, placing, contract, preferred_element_type=jnp.float32)


def prologue_kernel(
    count_ref, pos_ref, vel_ref, tau_ref, dest_ref, wpos_ref, wgam_ref, wcore_ref, *refs
):
    out_refs = refs[:-2]
    table_ref, state_ref = refs[-2:]
    regions = len(out_refs)
    capacity = out_refs[0].shape[1]
    per_device = dest_ref.shape[1]
    target = dest_ref[...]
    region_id = lax.broadcasted_iota(jnp.int32, (regions, per_device), 0)
    onehot = (target == region_id).astype(jnp.float32)
    row = lax.broadcasted_iota(jnp.int32, (per_device, per_device), 0)
    col = lax.broadcasted_iota(jnp.int32, (per_device, per_device), 1)
    upper = (row < col).astype(jnp.bfloat16)
    before = jnp.dot(onehot.astype(jnp.bfloat16), upper, preferred_element_type=jnp.float32)
    slot_rank = jnp.sum(before * onehot, axis=0, keepdims=True).astype(jnp.int32)
    column = target * capacity + slot_rank
    live = lax.broadcasted_iota(jnp.int32, (1, per_device), 1) < count_ref[0]
    state_ref[0:3, :] = pos_ref[...]
    state_ref[3:6, :] = vel_ref[...]
    state_ref[6:7, :] = tau_ref[...]
    state_ref[7:8, :] = jnp.ones((1, per_device), jnp.float32)
    state = state_ref[...]
    region = lax.axis_index("region")

    for shift, out_ref in enumerate(out_refs):
        dest_region = (region + shift) % regions
        slot_id = lax.broadcasted_iota(jnp.int32, (capacity, per_device), 0) + dest_region * capacity
        placing = ((column == slot_id) & live).astype(jnp.bfloat16)
        out_ref[...] = exact_place(state, placing)
    core = wcore_ref[...]
    table_ref[0:3, :] = wpos_ref[...]
    table_ref[3:4, :] = core * core
    table_ref[4:7, :] = wgam_ref[...]


def prologue(dust_pos, dust_vel, dust_tau, dest, counts, wake_pos, wake_gamma, wake_core):
    per_device = dust_tau.shape[0]
    regions = lax.axis_size("region")
    capacity = 2 * per_device // regions
    wake_count = wake_core.shape[0]
    vmem = pl.BlockSpec(memory_space=pltpu.VMEM)
    return pl.pallas_call(
        prologue_kernel,
        out_shape=tuple(
            [jax.ShapeDtypeStruct((8, capacity), jnp.float32)] * regions
            + [jax.ShapeDtypeStruct((7, wake_count), jnp.float32)]
        ),
        in_specs=[pl.BlockSpec(memory_space=pltpu.SMEM)] + [vmem] * 7,
        out_specs=tuple([vmem] * (regions + 1)),
        scratch_shapes=[pltpu.VMEM((8, per_device), jnp.float32)],
    )(
        counts, dust_pos, dust_vel, dust_tau.reshape(1, per_device), dest.reshape(1, per_device),
        wake_pos, wake_gamma, wake_core.reshape(1, wake_count),
    )


def exchange_slots(by_offset):
    regions = len(by_offset)
    rows, capacity = by_offset[0].shape
    region = lax.axis_index("region")
    if regions > 8:
        by_offset = jnp.stack(by_offset)
        back = (jnp.arange(regions, dtype=jnp.int32) - region) % regions
        blocks = jnp.take(by_offset, back, axis=0)
        arrived = lax.all_to_all(blocks, "region", split_axis=0, concat_axis=0, tiled=True)
        return arrived.transpose(1, 0, 2).reshape(rows, regions * capacity)
    by_shift = [by_offset[0]]
    for shift in range(1, regions):
        pairs = [(i, (i + shift) % regions) for i in range(regions)]
        by_shift.append(lax.ppermute(by_offset[shift], "region", pairs))
    placed = []
    for source in range(regions):
        shift = (region - source) % regions
        block = by_shift[0]
        for other in range(1, regions):
            block = jnp.where(shift == other, by_shift[other], block)
        placed.append(block)
    return jnp.concatenate(placed, axis=1)


def wake_tables(gathered):
    place = gathered[0:3]
    gamma = gathered[4:7]
    return jnp.concatenate([gathered, cross_rows(gamma, place)], axis=0)


def body(dust_pos, dust_vel, dust_tau, dest, counts, wake_pos, wake_gamma, wake_core):
    *outgoing, wake_table = prologue(
        dust_pos, dust_vel, dust_tau, dest, counts, wake_pos, wake_gamma, wake_core
    )
    outgoing, wake_table = lax.optimization_barrier((tuple(outgoing), wake_table))
    arrived = exchange_slots(outgoing)
    region_table = wake_tables(lax.all_gather(wake_table, "narrow", axis=1, tiled=True))
    points = arrived[0:3]
    raw_sums = raw_terms(points, region_table)
    return advance(arrived, raw_sums)


def solution(mesh):
    in_specs = (
        P(None, ("region", "narrow")),
        P(None, ("region", "narrow")),
        P(("region", "narrow")),
        P(("region", "narrow"), None),
        P(("region", "narrow")),
        P(None, ("region", "narrow")),
        P(None, ("region", "narrow")),
        P(("region", "narrow")),
    )
    out_specs = P(None, ("region", "narrow"))
    return jax.shard_map(body, mesh=mesh, in_specs=in_specs, out_specs=out_specs, check_vma=False)
```

```python
import functools
import math

import jax
import jax.numpy as jnp
from jax import lax
from jax.experimental import pallas as pl
from jax.experimental.pallas import tpu as pltpu
from jax.sharding import PartitionSpec as P

step_size = 0.1
gravity = 1.0


def cross_rows(first, second):
    return jnp.stack(
        [
            first[1] * second[2] - first[2] * second[1],
            first[2] * second[0] - first[0] * second[2],
            first[0] * second[1] - first[1] * second[0],
        ]
    )


def raw_terms(points, wake_table):
    point_count = points.shape[1]
    wake_count = wake_table.shape[1]
    wake_width = math.gcd(wake_count, 4096)
    wake_place = wake_table[0:3]
    core_square = wake_table[3]
    tables = wake_table[4:10]
    wake_offset = (
        wake_place[0] * wake_place[0]
        + wake_place[1] * wake_place[1]
        + wake_place[2] * wake_place[2]
        + core_square
    )
    place_blocks = (-2.0 * wake_place).reshape(3, wake_count // wake_width, wake_width).transpose(1, 0, 2)
    table_blocks = tables.reshape(6, wake_count // wake_width, wake_width).transpose(1, 0, 2)
    core_blocks = wake_offset.reshape(wake_count // wake_width, wake_width)
    point_blocks = points.reshape(3, point_count // point_count, point_count).transpose(1, 0, 2)

    def one_block(point_group):
        point_sq = (
            point_group[0] * point_group[0]
            + point_group[1] * point_group[1]
            + point_group[2] * point_group[2]
        )

        def accumulate(running, parts):
            scaled_place, table_part, offset_part = parts
            distance_sq = (
                (point_sq[:, None] + offset_part[None, :])
                + point_group[0][:, None] * scaled_place[0][None, :]
                + point_group[1][:, None] * scaled_place[1][None, :]
                + point_group[2][:, None] * scaled_place[2][None, :]
            )
            inverse_root = lax.rsqrt(distance_sq)
            kernel = inverse_root * inverse_root * inverse_root
            product = lax.dot_general(
                table_part, kernel, (((1,), (1,)), ((), ())), precision=lax.Precision.HIGH
            )
            return (running + product, None)

        total, _ = lax.scan(
            accumulate,
            jnp.zeros((6, point_count), jnp.float32),
            (place_blocks, table_blocks, core_blocks),
        )
        return total

    result = lax.map(one_block, point_blocks)
    return result.transpose(1, 0, 2).reshape(6, point_count)


def advance(arrived, raw_sums):
    points = arrived[0:3]
    velocity = arrived[3:6]
    live_flag = arrived[7]
    wind = (cross_rows(raw_sums[0:3], points) - raw_sums[3:6]) / (4.0 * math.pi)
    safe_tau = jnp.where(live_flag > 0.5, arrived[6], 1.0)
    rate = step_size / safe_tau
    upward = jnp.array([0.0, 0.0, 1.0], jnp.float32)[:, None]
    new_velocity = (velocity + rate[None, :] * wind - step_size * gravity * upward) / (
        1.0 + rate[None, :]
    )
    new_place = points + step_size * new_velocity
    return jnp.concatenate([new_place, new_velocity], axis=0) * live_flag[None, :]


def exact_place(values, placing):
    high = values.astype(jnp.bfloat16)
    rest = values - high.astype(jnp.float32)
    middle = rest.astype(jnp.bfloat16)
    low = (rest - middle.astype(jnp.float32)).astype(jnp.bfloat16)
    contract = (((1,), (1,)), ((), ()))
    total = lax.dot_general(high, placing, contract, preferred_element_type=jnp.float32)
    total = total + lax.dot_general(middle, placing, contract, preferred_element_type=jnp.float32)
    return total + lax.dot_general(low, placing, contract, preferred_element_type=jnp.float32)


def prologue_kernel(
    count_ref, pos_ref, vel_ref, tau_ref, dest_ref, wpos_ref, wgam_ref, wcore_ref, *refs
):
    out_refs = refs[:-2]
    table_ref, state_ref = refs[-2:]
    regions = len(out_refs)
    capacity = out_refs[0].shape[1]
    per_device = dest_ref.shape[1]
    target = dest_ref[...]
    region_id = lax.broadcasted_iota(jnp.int32, (regions, per_device), 0)
    onehot = (target == region_id).astype(jnp.float32)
    row = lax.broadcasted_iota(jnp.int32, (per_device, per_device), 0)
    col = lax.broadcasted_iota(jnp.int32, (per_device, per_device), 1)
    upper = (row < col).astype(jnp.bfloat16)
    before = jnp.dot(onehot.astype(jnp.bfloat16), upper, preferred_element_type=jnp.float32)
    slot_rank = jnp.sum(before * onehot, axis=0, keepdims=True).astype(jnp.int32)
    column = target * capacity + slot_rank
    live = lax.broadcasted_iota(jnp.int32, (1, per_device), 1) < count_ref[0]
    state_ref[0:3, :] = pos_ref[...]
    state_ref[3:6, :] = vel_ref[...]
    state_ref[6:7, :] = tau_ref[...]
    state_ref[7:8, :] = jnp.ones((1, per_device), jnp.float32)
    state = state_ref[...]
    region = lax.axis_index("region")

    for shift, out_ref in enumerate(out_refs):
        dest_region = (region + shift) % regions
        slot_id = lax.broadcasted_iota(jnp.int32, (capacity, per_device), 0) + dest_region * capacity
        placing = ((column == slot_id) & live).astype(jnp.bfloat16)
        out_ref[...] = exact_place(state, placing)
    core = wcore_ref[...]
    table_ref[0:3, :] = wpos_ref[...]
    table_ref[3:4, :] = core * core
    table_ref[4:7, :] = wgam_ref[...]


def prologue(dust_pos, dust_vel, dust_tau, dest, counts, wake_pos, wake_gamma, wake_core):
    per_device = dust_tau.shape[0]
    regions = lax.axis_size("region")
    capacity = 2 * per_device // regions
    wake_count = wake_core.shape[0]
    vmem = pl.BlockSpec(memory_space=pltpu.VMEM)
    return pl.pallas_call(
        prologue_kernel,
        out_shape=tuple(
            [jax.ShapeDtypeStruct((8, capacity), jnp.float32)] * regions
            + [jax.ShapeDtypeStruct((7, wake_count), jnp.float32)]
        ),
        in_specs=[pl.BlockSpec(memory_space=pltpu.SMEM)] + [vmem] * 7,
        out_specs=tuple([vmem] * (regions + 1)),
        scratch_shapes=[pltpu.VMEM((8, per_device), jnp.float32)],
    )(
        counts, dust_pos, dust_vel, dust_tau.reshape(1, per_device), dest.reshape(1, per_device),
        wake_pos, wake_gamma, wake_core.reshape(1, wake_count),
    )


def exchange_slots(by_offset):
    regions = len(by_offset)
    rows, capacity = by_offset[0].shape
    region = lax.axis_index("region")
    if regions > 8:
        by_offset = jnp.stack(by_offset)
        back = (jnp.arange(regions, dtype=jnp.int32) - region) % regions
        blocks = jnp.take(by_offset, back, axis=0)
        arrived = lax.all_to_all(blocks, "region", split_axis=0, concat_axis=0, tiled=True)
        return arrived.transpose(1, 0, 2).reshape(rows, regions * capacity)
    by_shift = [by_offset[0]]
    for shift in range(1, regions):
        pairs = [(i, (i + shift) % regions) for i in range(regions)]
        by_shift.append(lax.ppermute(by_offset[shift], "region", pairs))
    placed = []
    for source in range(regions):
        shift = (region - source) % regions
        block = by_shift[0]
        for other in range(1, regions):
            block = jnp.where(shift == other, by_shift[other], block)
        placed.append(block)
    return jnp.concatenate(placed, axis=1)


def wake_tables(gathered):
    place = gathered[0:3]
    gamma = gathered[4:7]
    return jnp.concatenate([gathered, cross_rows(gamma, place)], axis=0)


def body(dust_pos, dust_vel, dust_tau, dest, counts, wake_pos, wake_gamma, wake_core):
    *outgoing, wake_table = prologue(
        dust_pos, dust_vel, dust_tau, dest, counts, wake_pos, wake_gamma, wake_core
    )
    outgoing, wake_table = lax.optimization_barrier((tuple(outgoing), wake_table))
    arrived = exchange_slots(outgoing)
    region_table = wake_tables(lax.all_gather(wake_table, "narrow", axis=1, tiled=True))
    points = arrived[0:3]
    raw_sums = raw_terms(points, region_table)
    return advance(arrived, raw_sums)


def solution(mesh):
    in_specs = (
        P(None, ("region", "narrow")),
        P(None, ("region", "narrow")),
        P(("region", "narrow")),
        P(("region", "narrow"), None),
        P(("region", "narrow")),
        P(None, ("region", "narrow")),
        P(None, ("region", "narrow")),
        P(("region", "narrow")),
    )
    out_specs = P(None, ("region", "narrow"))
    return jax.shard_map(body, mesh=mesh, in_specs=in_specs, out_specs=out_specs, check_vma=False)
```

```python
import functools
import math

import jax
import jax.numpy as jnp
from jax import lax
from jax.experimental import pallas as pl
from jax.experimental.pallas import tpu as pltpu
from jax.sharding import PartitionSpec as P

step_size = 0.1
gravity = 1.0


def cross_rows(first, second):
    return jnp.stack(
        [
            first[1] * second[2] - first[2] * second[1],
            first[2] * second[0] - first[0] * second[2],
            first[0] * second[1] - first[1] * second[0],
        ]
    )


def raw_terms(points, wake_table):
    point_count = points.shape[1]
    wake_count = wake_table.shape[1]
    wake_width = math.gcd(wake_count, 8192)
    wake_place = wake_table[0:3]
    core_square = wake_table[3]
    tables = wake_table[4:10]
    wake_offset = (
        wake_place[0] * wake_place[0]
        + wake_place[1] * wake_place[1]
        + wake_place[2] * wake_place[2]
        + core_square
    )
    place_blocks = (-2.0 * wake_place).reshape(3, wake_count // wake_width, wake_width).transpose(1, 0, 2)
    table_blocks = tables.reshape(6, wake_count // wake_width, wake_width).transpose(1, 0, 2)
    core_blocks = wake_offset.reshape(wake_count // wake_width, wake_width)
    point_blocks = points.reshape(3, point_count // point_count, point_count).transpose(1, 0, 2)

    def one_block(point_group):
        point_sq = (
            point_group[0] * point_group[0]
            + point_group[1] * point_group[1]
            + point_group[2] * point_group[2]
        )

        def accumulate(running, parts):
            scaled_place, table_part, offset_part = parts
            distance_sq = (
                (point_sq[:, None] + offset_part[None, :])
                + point_group[0][:, None] * scaled_place[0][None, :]
                + point_group[1][:, None] * scaled_place[1][None, :]
                + point_group[2][:, None] * scaled_place[2][None, :]
            )
            inverse_root = lax.rsqrt(distance_sq)
            kernel = inverse_root * inverse_root * inverse_root
            product = lax.dot_general(
                table_part, kernel, (((1,), (1,)), ((), ())), precision=lax.Precision.HIGH
            )
            return (running + product, None)

        total, _ = lax.scan(
            accumulate,
            jnp.zeros((6, point_count), jnp.float32),
            (place_blocks, table_blocks, core_blocks),
        )
        return total

    result = lax.map(one_block, point_blocks)
    return result.transpose(1, 0, 2).reshape(6, point_count)


def advance(arrived, raw_sums):
    points = arrived[0:3]
    velocity = arrived[3:6]
    live_flag = arrived[7]
    wind = (cross_rows(raw_sums[0:3], points) - raw_sums[3:6]) / (4.0 * math.pi)
    safe_tau = jnp.where(live_flag > 0.5, arrived[6], 1.0)
    rate = step_size / safe_tau
    upward = jnp.array([0.0, 0.0, 1.0], jnp.float32)[:, None]
    new_velocity = (velocity + rate[None, :] * wind - step_size * gravity * upward) / (
        1.0 + rate[None, :]
    )
    new_place = points + step_size * new_velocity
    return jnp.concatenate([new_place, new_velocity], axis=0) * live_flag[None, :]


def exact_place(values, placing):
    high = values.astype(jnp.bfloat16)
    rest = values - high.astype(jnp.float32)
    middle = rest.astype(jnp.bfloat16)
    low = (rest - middle.astype(jnp.float32)).astype(jnp.bfloat16)
    contract = (((1,), (1,)), ((), ()))
    total = lax.dot_general(high, placing, contract, preferred_element_type=jnp.float32)
    total = total + lax.dot_general(middle, placing, contract, preferred_element_type=jnp.float32)
    return total + lax.dot_general(low, placing, contract, preferred_element_type=jnp.float32)


def prologue_kernel(
    count_ref, pos_ref, vel_ref, tau_ref, dest_ref, wpos_ref, wgam_ref, wcore_ref, *refs
):
    out_refs = refs[:-2]
    table_ref, state_ref = refs[-2:]
    regions = len(out_refs)
    capacity = out_refs[0].shape[1]
    per_device = dest_ref.shape[1]
    target = dest_ref[...]
    region_id = lax.broadcasted_iota(jnp.int32, (regions, per_device), 0)
    onehot = (target == region_id).astype(jnp.float32)
    row = lax.broadcasted_iota(jnp.int32, (per_device, per_device), 0)
    col = lax.broadcasted_iota(jnp.int32, (per_device, per_device), 1)
    upper = (row < col).astype(jnp.bfloat16)
    before = jnp.dot(onehot.astype(jnp.bfloat16), upper, preferred_element_type=jnp.float32)
    slot_rank = jnp.sum(before * onehot, axis=0, keepdims=True).astype(jnp.int32)
    column = target * capacity + slot_rank
    live = lax.broadcasted_iota(jnp.int32, (1, per_device), 1) < count_ref[0]
    state_ref[0:3, :] = pos_ref[...]
    state_ref[3:6, :] = vel_ref[...]
    state_ref[6:7, :] = tau_ref[...]
    state_ref[7:8, :] = jnp.ones((1, per_device), jnp.float32)
    state = state_ref[...]
    region = lax.axis_index("region")

    for shift, out_ref in enumerate(out_refs):
        dest_region = (region + shift) % regions
        slot_id = lax.broadcasted_iota(jnp.int32, (capacity, per_device), 0) + dest_region * capacity
        placing = ((column == slot_id) & live).astype(jnp.bfloat16)
        out_ref[...] = exact_place(state, placing)
    core = wcore_ref[...]
    table_ref[0:3, :] = wpos_ref[...]
    table_ref[3:4, :] = core * core
    table_ref[4:7, :] = wgam_ref[...]


def prologue(dust_pos, dust_vel, dust_tau, dest, counts, wake_pos, wake_gamma, wake_core):
    per_device = dust_tau.shape[0]
    regions = lax.axis_size("region")
    capacity = 2 * per_device // regions
    wake_count = wake_core.shape[0]
    vmem = pl.BlockSpec(memory_space=pltpu.VMEM)
    return pl.pallas_call(
        prologue_kernel,
        out_shape=tuple(
            [jax.ShapeDtypeStruct((8, capacity), jnp.float32)] * regions
            + [jax.ShapeDtypeStruct((7, wake_count), jnp.float32)]
        ),
        in_specs=[pl.BlockSpec(memory_space=pltpu.SMEM)] + [vmem] * 7,
        out_specs=tuple([vmem] * (regions + 1)),
        scratch_shapes=[pltpu.VMEM((8, per_device), jnp.float32)],
    )(
        counts, dust_pos, dust_vel, dust_tau.reshape(1, per_device), dest.reshape(1, per_device),
        wake_pos, wake_gamma, wake_core.reshape(1, wake_count),
    )


def exchange_slots(by_offset):
    regions = len(by_offset)
    rows, capacity = by_offset[0].shape
    region = lax.axis_index("region")
    if regions > 8:
        by_offset = jnp.stack(by_offset)
        back = (jnp.arange(regions, dtype=jnp.int32) - region) % regions
        blocks = jnp.take(by_offset, back, axis=0)
        arrived = lax.all_to_all(blocks, "region", split_axis=0, concat_axis=0, tiled=True)
        return arrived.transpose(1, 0, 2).reshape(rows, regions * capacity)
    by_shift = [by_offset[0]]
    for shift in range(1, regions):
        pairs = [(i, (i + shift) % regions) for i in range(regions)]
        by_shift.append(lax.ppermute(by_offset[shift], "region", pairs))
    placed = []
    for source in range(regions):
        shift = (region - source) % regions
        block = by_shift[0]
        for other in range(1, regions):
            block = jnp.where(shift == other, by_shift[other], block)
        placed.append(block)
    return jnp.concatenate(placed, axis=1)


def wake_tables(gathered):
    place = gathered[0:3]
    gamma = gathered[4:7]
    return jnp.concatenate([gathered, cross_rows(gamma, place)], axis=0)


def body(dust_pos, dust_vel, dust_tau, dest, counts, wake_pos, wake_gamma, wake_core):
    *outgoing, wake_table = prologue(
        dust_pos, dust_vel, dust_tau, dest, counts, wake_pos, wake_gamma, wake_core
    )
    outgoing, wake_table = lax.optimization_barrier((tuple(outgoing), wake_table))
    arrived = exchange_slots(outgoing)
    region_table = wake_tables(lax.all_gather(wake_table, "narrow", axis=1, tiled=True))
    points = arrived[0:3]
    raw_sums = raw_terms(points, region_table)
    return advance(arrived, raw_sums)


def solution(mesh):
    in_specs = (
        P(None, ("region", "narrow")),
        P(None, ("region", "narrow")),
        P(("region", "narrow")),
        P(("region", "narrow"), None),
        P(("region", "narrow")),
        P(None, ("region", "narrow")),
        P(None, ("region", "narrow")),
        P(("region", "narrow")),
    )
    out_specs = P(None, ("region", "narrow"))
    return jax.shard_map(body, mesh=mesh, in_specs=in_specs, out_specs=out_specs, check_vma=False)
```

```python
import functools
import math

import jax
import jax.numpy as jnp
from jax import lax
from jax.experimental import pallas as pl
from jax.experimental.pallas import tpu as pltpu
from jax.sharding import PartitionSpec as P

step_size = 0.1
gravity = 1.0


def cross_rows(first, second):
    return jnp.stack(
        [
            first[1] * second[2] - first[2] * second[1],
            first[2] * second[0] - first[0] * second[2],
            first[0] * second[1] - first[1] * second[0],
        ]
    )


def raw_terms(points, wake_table):
    point_count = points.shape[1]
    wake_count = wake_table.shape[1]
    wake_width = math.gcd(wake_count, 8192)
    wake_place = wake_table[0:3]
    core_square = wake_table[3]
    tables = wake_table[4:10]
    wake_offset = (
        wake_place[0] * wake_place[0]
        + wake_place[1] * wake_place[1]
        + wake_place[2] * wake_place[2]
        + core_square
    )
    place_blocks = (-2.0 * wake_place).reshape(3, wake_count // wake_width, wake_width).transpose(1, 0, 2)
    table_blocks = tables.reshape(6, wake_count // wake_width, wake_width).transpose(1, 0, 2)
    core_blocks = wake_offset.reshape(wake_count // wake_width, wake_width)
    point_width = point_count // 2 if point_count % 256 == 128 else point_count
    point_blocks = points.reshape(3, point_count // point_width, point_width).transpose(1, 0, 2)

    def one_block(point_group):
        point_sq = (
            point_group[0] * point_group[0]
            + point_group[1] * point_group[1]
            + point_group[2] * point_group[2]
        )

        def accumulate(running, parts):
            scaled_place, table_part, offset_part = parts
            distance_sq = (
                (point_sq[:, None] + offset_part[None, :])
                + point_group[0][:, None] * scaled_place[0][None, :]
                + point_group[1][:, None] * scaled_place[1][None, :]
                + point_group[2][:, None] * scaled_place[2][None, :]
            )
            inverse_root = lax.rsqrt(distance_sq)
            kernel = inverse_root * inverse_root * inverse_root
            product = lax.dot_general(
                table_part, kernel, (((1,), (1,)), ((), ())), precision=lax.Precision.HIGH
            )
            return (running + product, None)

        total, _ = lax.scan(
            accumulate,
            jnp.zeros((6, point_width), jnp.float32),
            (place_blocks, table_blocks, core_blocks),
        )
        return total

    result = lax.map(one_block, point_blocks)
    return result.transpose(1, 0, 2).reshape(6, point_count)


def advance(arrived, raw_sums):
    points = arrived[0:3]
    velocity = arrived[3:6]
    live_flag = arrived[7]
    wind = (cross_rows(raw_sums[0:3], points) - raw_sums[3:6]) / (4.0 * math.pi)
    safe_tau = jnp.where(live_flag > 0.5, arrived[6], 1.0)
    rate = step_size / safe_tau
    upward = jnp.array([0.0, 0.0, 1.0], jnp.float32)[:, None]
    new_velocity = (velocity + rate[None, :] * wind - step_size * gravity * upward) / (
        1.0 + rate[None, :]
    )
    new_place = points + step_size * new_velocity
    return jnp.concatenate([new_place, new_velocity], axis=0) * live_flag[None, :]


def exact_place(values, placing):
    high = values.astype(jnp.bfloat16)
    rest = values - high.astype(jnp.float32)
    middle = rest.astype(jnp.bfloat16)
    low = (rest - middle.astype(jnp.float32)).astype(jnp.bfloat16)
    contract = (((1,), (1,)), ((), ()))
    total = lax.dot_general(high, placing, contract, preferred_element_type=jnp.float32)
    total = total + lax.dot_general(middle, placing, contract, preferred_element_type=jnp.float32)
    return total + lax.dot_general(low, placing, contract, preferred_element_type=jnp.float32)


def prologue_kernel(
    count_ref, pos_ref, vel_ref, tau_ref, dest_ref, wpos_ref, wgam_ref, wcore_ref, *refs
):
    out_refs = refs[:-2]
    table_ref, state_ref = refs[-2:]
    regions = len(out_refs)
    capacity = out_refs[0].shape[1]
    per_device = dest_ref.shape[1]
    target = dest_ref[...]
    region_id = lax.broadcasted_iota(jnp.int32, (regions, per_device), 0)
    onehot = (target == region_id).astype(jnp.float32)
    row = lax.broadcasted_iota(jnp.int32, (per_device, per_device), 0)
    col = lax.broadcasted_iota(jnp.int32, (per_device, per_device), 1)
    upper = (row < col).astype(jnp.bfloat16)
    before = jnp.dot(onehot.astype(jnp.bfloat16), upper, preferred_element_type=jnp.float32)
    slot_rank = jnp.sum(before * onehot, axis=0, keepdims=True).astype(jnp.int32)
    column = target * capacity + slot_rank
    live = lax.broadcasted_iota(jnp.int32, (1, per_device), 1) < count_ref[0]
    state_ref[0:3, :] = pos_ref[...]
    state_ref[3:6, :] = vel_ref[...]
    state_ref[6:7, :] = tau_ref[...]
    state_ref[7:8, :] = jnp.ones((1, per_device), jnp.float32)
    state = state_ref[...]
    region = lax.axis_index("region")

    for shift, out_ref in enumerate(out_refs):
        dest_region = (region + shift) % regions
        slot_id = lax.broadcasted_iota(jnp.int32, (capacity, per_device), 0) + dest_region * capacity
        placing = ((column == slot_id) & live).astype(jnp.bfloat16)
        out_ref[...] = exact_place(state, placing)
    core = wcore_ref[...]
    table_ref[0:3, :] = wpos_ref[...]
    table_ref[3:4, :] = core * core
    table_ref[4:7, :] = wgam_ref[...]


def prologue(dust_pos, dust_vel, dust_tau, dest, counts, wake_pos, wake_gamma, wake_core):
    per_device = dust_tau.shape[0]
    regions = lax.axis_size("region")
    capacity = 2 * per_device // regions
    wake_count = wake_core.shape[0]
    vmem = pl.BlockSpec(memory_space=pltpu.VMEM)
    return pl.pallas_call(
        prologue_kernel,
        out_shape=tuple(
            [jax.ShapeDtypeStruct((8, capacity), jnp.float32)] * regions
            + [jax.ShapeDtypeStruct((7, wake_count), jnp.float32)]
        ),
        in_specs=[pl.BlockSpec(memory_space=pltpu.SMEM)] + [vmem] * 7,
        out_specs=tuple([vmem] * (regions + 1)),
        scratch_shapes=[pltpu.VMEM((8, per_device), jnp.float32)],
    )(
        counts, dust_pos, dust_vel, dust_tau.reshape(1, per_device), dest.reshape(1, per_device),
        wake_pos, wake_gamma, wake_core.reshape(1, wake_count),
    )


def exchange_slots(by_offset):
    regions = len(by_offset)
    rows, capacity = by_offset[0].shape
    region = lax.axis_index("region")
    if regions > 8:
        by_offset = jnp.stack(by_offset)
        back = (jnp.arange(regions, dtype=jnp.int32) - region) % regions
        blocks = jnp.take(by_offset, back, axis=0)
        arrived = lax.all_to_all(blocks, "region", split_axis=0, concat_axis=0, tiled=True)
        return arrived.transpose(1, 0, 2).reshape(rows, regions * capacity)
    by_shift = [by_offset[0]]
    for shift in range(1, regions):
        pairs = [(i, (i + shift) % regions) for i in range(regions)]
        by_shift.append(lax.ppermute(by_offset[shift], "region", pairs))
    placed = []
    for source in range(regions):
        shift = (region - source) % regions
        block = by_shift[0]
        for other in range(1, regions):
            block = jnp.where(shift == other, by_shift[other], block)
        placed.append(block)
    return jnp.concatenate(placed, axis=1)


def wake_tables(gathered):
    place = gathered[0:3]
    gamma = gathered[4:7]
    return jnp.concatenate([gathered, cross_rows(gamma, place)], axis=0)


def body(dust_pos, dust_vel, dust_tau, dest, counts, wake_pos, wake_gamma, wake_core):
    *outgoing, wake_table = prologue(
        dust_pos, dust_vel, dust_tau, dest, counts, wake_pos, wake_gamma, wake_core
    )
    outgoing, wake_table = lax.optimization_barrier((tuple(outgoing), wake_table))
    arrived = exchange_slots(outgoing)
    region_table = wake_tables(lax.all_gather(wake_table, "narrow", axis=1, tiled=True))
    points = arrived[0:3]
    raw_sums = raw_terms(points, region_table)
    return advance(arrived, raw_sums)


def solution(mesh):
    in_specs = (
        P(None, ("region", "narrow")),
        P(None, ("region", "narrow")),
        P(("region", "narrow")),
        P(("region", "narrow"), None),
        P(("region", "narrow")),
        P(None, ("region", "narrow")),
        P(None, ("region", "narrow")),
        P(("region", "narrow")),
    )
    out_specs = P(None, ("region", "narrow"))
    return jax.shard_map(body, mesh=mesh, in_specs=in_specs, out_specs=out_specs, check_vma=False)
```

```python
import functools
import math

import jax
import jax.numpy as jnp
from jax import lax
from jax.experimental import pallas as pl
from jax.experimental.pallas import tpu as pltpu
from jax.sharding import PartitionSpec as P

step_size = 0.1
gravity = 1.0


def cross_rows(first, second):
    return jnp.stack(
        [
            first[1] * second[2] - first[2] * second[1],
            first[2] * second[0] - first[0] * second[2],
            first[0] * second[1] - first[1] * second[0],
        ]
    )


def raw_terms(points, wake_table):
    point_count = points.shape[1]
    wake_count = wake_table.shape[1]
    wake_width = math.gcd(wake_count, 8192)
    wake_place = wake_table[0:3]
    core_square = wake_table[3]
    tables = wake_table[4:10]
    wake_offset = (
        wake_place[0] * wake_place[0]
        + wake_place[1] * wake_place[1]
        + wake_place[2] * wake_place[2]
        + core_square
    )
    place_blocks = (-2.0 * wake_place).reshape(3, wake_count // wake_width, wake_width).transpose(1, 0, 2)
    table_blocks = tables.reshape(6, wake_count // wake_width, wake_width).transpose(1, 0, 2)
    core_blocks = wake_offset.reshape(wake_count // wake_width, wake_width)
    point_blocks = points.reshape(3, point_count // point_count, point_count).transpose(1, 0, 2)

    def one_block(point_group):
        point_sq = (
            point_group[0] * point_group[0]
            + point_group[1] * point_group[1]
            + point_group[2] * point_group[2]
        )

        def accumulate(running, parts):
            scaled_place, table_part, offset_part = parts
            distance_sq = (
                (offset_part[:, None] + point_sq[None, :])
                + scaled_place[0][:, None] * point_group[0][None, :]
                + scaled_place[1][:, None] * point_group[1][None, :]
                + scaled_place[2][:, None] * point_group[2][None, :]
            )
            inverse_root = lax.rsqrt(distance_sq)
            kernel = inverse_root * inverse_root * inverse_root
            product = lax.dot_general(
                table_part, kernel, (((1,), (0,)), ((), ())), precision=lax.Precision.HIGH
            )
            return (running + product, None)

        total, _ = lax.scan(
            accumulate,
            jnp.zeros((6, point_count), jnp.float32),
            (place_blocks, table_blocks, core_blocks),
        )
        return total

    result = lax.map(one_block, point_blocks)
    return result.transpose(1, 0, 2).reshape(6, point_count)


def advance(arrived, raw_sums):
    points = arrived[0:3]
    velocity = arrived[3:6]
    live_flag = arrived[7]
    wind = (cross_rows(raw_sums[0:3], points) - raw_sums[3:6]) / (4.0 * math.pi)
    safe_tau = jnp.where(live_flag > 0.5, arrived[6], 1.0)
    rate = step_size / safe_tau
    upward = jnp.array([0.0, 0.0, 1.0], jnp.float32)[:, None]
    new_velocity = (velocity + rate[None, :] * wind - step_size * gravity * upward) / (
        1.0 + rate[None, :]
    )
    new_place = points + step_size * new_velocity
    return jnp.concatenate([new_place, new_velocity], axis=0) * live_flag[None, :]


def exact_place(values, placing):
    high = values.astype(jnp.bfloat16)
    rest = values - high.astype(jnp.float32)
    middle = rest.astype(jnp.bfloat16)
    low = (rest - middle.astype(jnp.float32)).astype(jnp.bfloat16)
    contract = (((1,), (1,)), ((), ()))
    total = lax.dot_general(high, placing, contract, preferred_element_type=jnp.float32)
    total = total + lax.dot_general(middle, placing, contract, preferred_element_type=jnp.float32)
    return total + lax.dot_general(low, placing, contract, preferred_element_type=jnp.float32)


def prologue_kernel(
    count_ref, pos_ref, vel_ref, tau_ref, dest_ref, wpos_ref, wgam_ref, wcore_ref, *refs
):
    out_refs = refs[:-2]
    table_ref, state_ref = refs[-2:]
    regions = len(out_refs)
    capacity = out_refs[0].shape[1]
    per_device = dest_ref.shape[1]
    target = dest_ref[...]
    region_id = lax.broadcasted_iota(jnp.int32, (regions, per_device), 0)
    onehot = (target == region_id).astype(jnp.float32)
    row = lax.broadcasted_iota(jnp.int32, (per_device, per_device), 0)
    col = lax.broadcasted_iota(jnp.int32, (per_device, per_device), 1)
    upper = (row < col).astype(jnp.bfloat16)
    before = jnp.dot(onehot.astype(jnp.bfloat16), upper, preferred_element_type=jnp.float32)
    slot_rank = jnp.sum(before * onehot, axis=0, keepdims=True).astype(jnp.int32)
    column = target * capacity + slot_rank
    live = lax.broadcasted_iota(jnp.int32, (1, per_device), 1) < count_ref[0]
    state_ref[0:3, :] = pos_ref[...]
    state_ref[3:6, :] = vel_ref[...]
    state_ref[6:7, :] = tau_ref[...]
    state_ref[7:8, :] = jnp.ones((1, per_device), jnp.float32)
    state = state_ref[...]
    region = lax.axis_index("region")

    for shift, out_ref in enumerate(out_refs):
        dest_region = (region + shift) % regions
        slot_id = lax.broadcasted_iota(jnp.int32, (capacity, per_device), 0) + dest_region * capacity
        placing = ((column == slot_id) & live).astype(jnp.bfloat16)
        out_ref[...] = exact_place(state, placing)
    core = wcore_ref[...]
    table_ref[0:3, :] = wpos_ref[...]
    table_ref[3:4, :] = core * core
    table_ref[4:7, :] = wgam_ref[...]


def prologue(dust_pos, dust_vel, dust_tau, dest, counts, wake_pos, wake_gamma, wake_core):
    per_device = dust_tau.shape[0]
    regions = lax.axis_size("region")
    capacity = 2 * per_device // regions
    wake_count = wake_core.shape[0]
    vmem = pl.BlockSpec(memory_space=pltpu.VMEM)
    return pl.pallas_call(
        prologue_kernel,
        out_shape=tuple(
            [jax.ShapeDtypeStruct((8, capacity), jnp.float32)] * regions
            + [jax.ShapeDtypeStruct((7, wake_count), jnp.float32)]
        ),
        in_specs=[pl.BlockSpec(memory_space=pltpu.SMEM)] + [vmem] * 7,
        out_specs=tuple([vmem] * (regions + 1)),
        scratch_shapes=[pltpu.VMEM((8, per_device), jnp.float32)],
    )(
        counts, dust_pos, dust_vel, dust_tau.reshape(1, per_device), dest.reshape(1, per_device),
        wake_pos, wake_gamma, wake_core.reshape(1, wake_count),
    )


def exchange_slots(by_offset):
    regions = len(by_offset)
    rows, capacity = by_offset[0].shape
    region = lax.axis_index("region")
    if regions > 8:
        by_offset = jnp.stack(by_offset)
        back = (jnp.arange(regions, dtype=jnp.int32) - region) % regions
        blocks = jnp.take(by_offset, back, axis=0)
        arrived = lax.all_to_all(blocks, "region", split_axis=0, concat_axis=0, tiled=True)
        return arrived.transpose(1, 0, 2).reshape(rows, regions * capacity)
    by_shift = [by_offset[0]]
    for shift in range(1, regions):
        pairs = [(i, (i + shift) % regions) for i in range(regions)]
        by_shift.append(lax.ppermute(by_offset[shift], "region", pairs))
    placed = []
    for source in range(regions):
        shift = (region - source) % regions
        block = by_shift[0]
        for other in range(1, regions):
            block = jnp.where(shift == other, by_shift[other], block)
        placed.append(block)
    return jnp.concatenate(placed, axis=1)


def wake_tables(gathered):
    place = gathered[0:3]
    gamma = gathered[4:7]
    return jnp.concatenate([gathered, cross_rows(gamma, place)], axis=0)


def body(dust_pos, dust_vel, dust_tau, dest, counts, wake_pos, wake_gamma, wake_core):
    *outgoing, wake_table = prologue(
        dust_pos, dust_vel, dust_tau, dest, counts, wake_pos, wake_gamma, wake_core
    )
    outgoing, wake_table = lax.optimization_barrier((tuple(outgoing), wake_table))
    arrived = exchange_slots(outgoing)
    region_table = wake_tables(lax.all_gather(wake_table, "narrow", axis=1, tiled=True))
    points = arrived[0:3]
    raw_sums = raw_terms(points, region_table)
    return advance(arrived, raw_sums)


def solution(mesh):
    in_specs = (
        P(None, ("region", "narrow")),
        P(None, ("region", "narrow")),
        P(("region", "narrow")),
        P(("region", "narrow"), None),
        P(("region", "narrow")),
        P(None, ("region", "narrow")),
        P(None, ("region", "narrow")),
        P(("region", "narrow")),
    )
    out_specs = P(None, ("region", "narrow"))
    return jax.shard_map(body, mesh=mesh, in_specs=in_specs, out_specs=out_specs, check_vma=False)
```

```python
import functools
import math

import jax
import jax.numpy as jnp
from jax import lax
from jax.experimental import pallas as pl
from jax.experimental.pallas import tpu as pltpu
from jax.sharding import PartitionSpec as P

step_size = 0.1
gravity = 1.0


def cross_rows(first, second):
    return jnp.stack(
        [
            first[1] * second[2] - first[2] * second[1],
            first[2] * second[0] - first[0] * second[2],
            first[0] * second[1] - first[1] * second[0],
        ]
    )


def raw_terms(points, wake_table):
    point_count = points.shape[1]
    wake_count = wake_table.shape[1]
    wake_width = math.gcd(wake_count, 4096)
    wake_place = wake_table[0:3]
    core_square = wake_table[3]
    tables = wake_table[4:10]
    wake_offset = (
        wake_place[0] * wake_place[0]
        + wake_place[1] * wake_place[1]
        + wake_place[2] * wake_place[2]
        + core_square
    )
    place_blocks = (-2.0 * wake_place).reshape(3, wake_count // wake_width, wake_width).transpose(1, 0, 2)
    table_blocks = tables.reshape(6, wake_count // wake_width, wake_width).transpose(1, 0, 2)
    core_blocks = wake_offset.reshape(wake_count // wake_width, wake_width)
    point_blocks = points.reshape(3, point_count // point_count, point_count).transpose(1, 0, 2)

    def one_block(point_group):
        point_sq = (
            point_group[0] * point_group[0]
            + point_group[1] * point_group[1]
            + point_group[2] * point_group[2]
        )

        def accumulate(running, parts):
            scaled_place, table_part, offset_part = parts
            distance_sq = (
                (offset_part[:, None] + point_sq[None, :])
                + scaled_place[0][:, None] * point_group[0][None, :]
                + scaled_place[1][:, None] * point_group[1][None, :]
                + scaled_place[2][:, None] * point_group[2][None, :]
            )
            inverse_root = lax.rsqrt(distance_sq)
            kernel = inverse_root * inverse_root * inverse_root
            product = lax.dot_general(
                table_part, kernel, (((1,), (0,)), ((), ())), precision=lax.Precision.HIGH
            )
            return (running + product, None)

        total, _ = lax.scan(
            accumulate,
            jnp.zeros((6, point_count), jnp.float32),
            (place_blocks, table_blocks, core_blocks),
        )
        return total

    result = lax.map(one_block, point_blocks)
    return result.transpose(1, 0, 2).reshape(6, point_count)


def advance(arrived, raw_sums):
    points = arrived[0:3]
    velocity = arrived[3:6]
    live_flag = arrived[7]
    wind = (cross_rows(raw_sums[0:3], points) - raw_sums[3:6]) / (4.0 * math.pi)
    safe_tau = jnp.where(live_flag > 0.5, arrived[6], 1.0)
    rate = step_size / safe_tau
    upward = jnp.array([0.0, 0.0, 1.0], jnp.float32)[:, None]
    new_velocity = (velocity + rate[None, :] * wind - step_size * gravity * upward) / (
        1.0 + rate[None, :]
    )
    new_place = points + step_size * new_velocity
    return jnp.concatenate([new_place, new_velocity], axis=0) * live_flag[None, :]


def exact_place(values, placing):
    high = values.astype(jnp.bfloat16)
    rest = values - high.astype(jnp.float32)
    middle = rest.astype(jnp.bfloat16)
    low = (rest - middle.astype(jnp.float32)).astype(jnp.bfloat16)
    contract = (((1,), (1,)), ((), ()))
    total = lax.dot_general(high, placing, contract, preferred_element_type=jnp.float32)
    total = total + lax.dot_general(middle, placing, contract, preferred_element_type=jnp.float32)
    return total + lax.dot_general(low, placing, contract, preferred_element_type=jnp.float32)


def prologue_kernel(
    count_ref, pos_ref, vel_ref, tau_ref, dest_ref, wpos_ref, wgam_ref, wcore_ref, *refs
):
    out_refs = refs[:-2]
    table_ref, state_ref = refs[-2:]
    regions = len(out_refs)
    capacity = out_refs[0].shape[1]
    per_device = dest_ref.shape[1]
    target = dest_ref[...]
    region_id = lax.broadcasted_iota(jnp.int32, (regions, per_device), 0)
    onehot = (target == region_id).astype(jnp.float32)
    row = lax.broadcasted_iota(jnp.int32, (per_device, per_device), 0)
    col = lax.broadcasted_iota(jnp.int32, (per_device, per_device), 1)
    upper = (row < col).astype(jnp.bfloat16)
    before = jnp.dot(onehot.astype(jnp.bfloat16), upper, preferred_element_type=jnp.float32)
    slot_rank = jnp.sum(before * onehot, axis=0, keepdims=True).astype(jnp.int32)
    column = target * capacity + slot_rank
    live = lax.broadcasted_iota(jnp.int32, (1, per_device), 1) < count_ref[0]
    state_ref[0:3, :] = pos_ref[...]
    state_ref[3:6, :] = vel_ref[...]
    state_ref[6:7, :] = tau_ref[...]
    state_ref[7:8, :] = jnp.ones((1, per_device), jnp.float32)
    state = state_ref[...]
    region = lax.axis_index("region")

    for shift, out_ref in enumerate(out_refs):
        dest_region = (region + shift) % regions
        slot_id = lax.broadcasted_iota(jnp.int32, (capacity, per_device), 0) + dest_region * capacity
        placing = ((column == slot_id) & live).astype(jnp.bfloat16)
        out_ref[...] = exact_place(state, placing)
    core = wcore_ref[...]
    table_ref[0:3, :] = wpos_ref[...]
    table_ref[3:4, :] = core * core
    table_ref[4:7, :] = wgam_ref[...]


def prologue(dust_pos, dust_vel, dust_tau, dest, counts, wake_pos, wake_gamma, wake_core):
    per_device = dust_tau.shape[0]
    regions = lax.axis_size("region")
    capacity = 2 * per_device // regions
    wake_count = wake_core.shape[0]
    vmem = pl.BlockSpec(memory_space=pltpu.VMEM)
    return pl.pallas_call(
        prologue_kernel,
        out_shape=tuple(
            [jax.ShapeDtypeStruct((8, capacity), jnp.float32)] * regions
            + [jax.ShapeDtypeStruct((7, wake_count), jnp.float32)]
        ),
        in_specs=[pl.BlockSpec(memory_space=pltpu.SMEM)] + [vmem] * 7,
        out_specs=tuple([vmem] * (regions + 1)),
        scratch_shapes=[pltpu.VMEM((8, per_device), jnp.float32)],
    )(
        counts, dust_pos, dust_vel, dust_tau.reshape(1, per_device), dest.reshape(1, per_device),
        wake_pos, wake_gamma, wake_core.reshape(1, wake_count),
    )


def exchange_slots(by_offset):
    regions = len(by_offset)
    rows, capacity = by_offset[0].shape
    region = lax.axis_index("region")
    if regions > 8:
        by_offset = jnp.stack(by_offset)
        back = (jnp.arange(regions, dtype=jnp.int32) - region) % regions
        blocks = jnp.take(by_offset, back, axis=0)
        arrived = lax.all_to_all(blocks, "region", split_axis=0, concat_axis=0, tiled=True)
        return arrived.transpose(1, 0, 2).reshape(rows, regions * capacity)
    by_shift = [by_offset[0]]
    for shift in range(1, regions):
        pairs = [(i, (i + shift) % regions) for i in range(regions)]
        by_shift.append(lax.ppermute(by_offset[shift], "region", pairs))
    placed = []
    for source in range(regions):
        shift = (region - source) % regions
        block = by_shift[0]
        for other in range(1, regions):
            block = jnp.where(shift == other, by_shift[other], block)
        placed.append(block)
    return jnp.concatenate(placed, axis=1)


def wake_tables(gathered):
    place = gathered[0:3]
    gamma = gathered[4:7]
    return jnp.concatenate([gathered, cross_rows(gamma, place)], axis=0)


def body(dust_pos, dust_vel, dust_tau, dest, counts, wake_pos, wake_gamma, wake_core):
    *outgoing, wake_table = prologue(
        dust_pos, dust_vel, dust_tau, dest, counts, wake_pos, wake_gamma, wake_core
    )
    outgoing, wake_table = lax.optimization_barrier((tuple(outgoing), wake_table))
    arrived = exchange_slots(outgoing)
    region_table = wake_tables(lax.all_gather(wake_table, "narrow", axis=1, tiled=True))
    points = arrived[0:3]
    raw_sums = raw_terms(points, region_table)
    return advance(arrived, raw_sums)


def solution(mesh):
    in_specs = (
        P(None, ("region", "narrow")),
        P(None, ("region", "narrow")),
        P(("region", "narrow")),
        P(("region", "narrow"), None),
        P(("region", "narrow")),
        P(None, ("region", "narrow")),
        P(None, ("region", "narrow")),
        P(("region", "narrow")),
    )
    out_specs = P(None, ("region", "narrow"))
    return jax.shard_map(body, mesh=mesh, in_specs=in_specs, out_specs=out_specs, check_vma=False)
```

```python
import functools
import math

import jax
import jax.numpy as jnp
from jax import lax
from jax.experimental import pallas as pl
from jax.experimental.pallas import tpu as pltpu
from jax.sharding import PartitionSpec as P

step_size = 0.1
gravity = 1.0


def cross_rows(first, second):
    return jnp.stack(
        [
            first[1] * second[2] - first[2] * second[1],
            first[2] * second[0] - first[0] * second[2],
            first[0] * second[1] - first[1] * second[0],
        ]
    )


def raw_terms(points, wake_table):
    point_count = points.shape[1]
    wake_count = wake_table.shape[1]
    wake_width = math.gcd(wake_count, 8192)
    wake_place = wake_table[0:3]
    core_square = wake_table[3]
    tables = wake_table[4:10]
    wake_offset = (
        wake_place[0] * wake_place[0]
        + wake_place[1] * wake_place[1]
        + wake_place[2] * wake_place[2]
        + core_square
    )
    place_blocks = (-2.0 * wake_place).reshape(3, wake_count // wake_width, wake_width).transpose(1, 0, 2)
    table_blocks = tables.reshape(6, wake_count // wake_width, wake_width).transpose(1, 0, 2)
    core_blocks = wake_offset.reshape(wake_count // wake_width, wake_width)
    point_blocks = points.reshape(3, point_count // point_count, point_count).transpose(1, 0, 2)

    def one_block(point_group):
        point_sq = (
            point_group[0] * point_group[0]
            + point_group[1] * point_group[1]
            + point_group[2] * point_group[2]
        )

        def accumulate(running, parts):
            scaled_place, table_part, offset_part = parts
            distance_sq = (
                (offset_part[:, None] + point_sq[None, :])
                + scaled_place[0][:, None] * point_group[0][None, :]
                + scaled_place[1][:, None] * point_group[1][None, :]
                + scaled_place[2][:, None] * point_group[2][None, :]
            )
            inverse_root = lax.rsqrt(distance_sq)
            kernel = inverse_root * inverse_root * inverse_root
            product = lax.dot_general(
                table_part, kernel, (((1,), (0,)), ((), ())), precision=lax.Precision.HIGH
            )
            return (running + product, None)

        total, _ = lax.scan(
            accumulate,
            jnp.zeros((6, point_count), jnp.float32),
            (place_blocks, table_blocks, core_blocks),
        )
        return total

    result = lax.map(one_block, point_blocks)
    return result.transpose(1, 0, 2).reshape(6, point_count)


def advance(arrived, raw_sums):
    points = arrived[0:3]
    velocity = arrived[3:6]
    live_flag = arrived[7]
    wind = (cross_rows(raw_sums[0:3], points) - raw_sums[3:6]) / (4.0 * math.pi)
    safe_tau = jnp.where(live_flag > 0.5, arrived[6], 1.0)
    rate = step_size / safe_tau
    upward = jnp.array([0.0, 0.0, 1.0], jnp.float32)[:, None]
    new_velocity = (velocity + rate[None, :] * wind - step_size * gravity * upward) / (
        1.0 + rate[None, :]
    )
    new_place = points + step_size * new_velocity
    return jnp.concatenate([new_place, new_velocity], axis=0) * live_flag[None, :]


def prologue_kernel(
    count_ref, pos_ref, vel_ref, tau_ref, dest_ref, wpos_ref, wgam_ref, wcore_ref, *refs
):
    out_refs = refs[:-2]
    table_ref, split_ref = refs[-2:]
    regions = len(out_refs)
    capacity = out_refs[0].shape[1]
    per_device = dest_ref.shape[1]
    target = dest_ref[...]
    region_id = lax.broadcasted_iota(jnp.int32, (regions, per_device), 0)
    onehot = (target == region_id).astype(jnp.float32)
    row = lax.broadcasted_iota(jnp.int32, (per_device, per_device), 0)
    col = lax.broadcasted_iota(jnp.int32, (per_device, per_device), 1)
    upper = (row < col).astype(jnp.bfloat16)
    before = jnp.dot(onehot.astype(jnp.bfloat16), upper, preferred_element_type=jnp.float32)
    slot_rank = jnp.sum(before * onehot, axis=0, keepdims=True).astype(jnp.int32)
    column = target * capacity + slot_rank
    live = lax.broadcasted_iota(jnp.int32, (1, per_device), 1) < count_ref[0]
    state = jnp.concatenate(
        [pos_ref[...], vel_ref[...], tau_ref[...], jnp.ones((1, per_device), jnp.float32)], axis=0
    )
    high = state.astype(jnp.bfloat16).astype(jnp.float32)
    rest = state - high
    middle = rest.astype(jnp.bfloat16).astype(jnp.float32)
    split_ref[0:8, :] = high
    split_ref[8:16, :] = middle
    split_ref[16:24, :] = rest - middle
    split = split_ref[...].astype(jnp.bfloat16)
    region = lax.axis_index("region")
    for shift, out_ref in enumerate(out_refs):
        dest_region = (region + shift) % regions
        slot_id = lax.broadcasted_iota(jnp.int32, (capacity, per_device), 0) + dest_region * capacity
        placing = ((column == slot_id) & live).astype(jnp.bfloat16)
        parts = lax.dot_general(
            split, placing, (((1,), (1,)), ((), ())), preferred_element_type=jnp.float32
        )
        out_ref[...] = (parts[0:8] + parts[8:16]) + parts[16:24]
    core = wcore_ref[...]
    table_ref[0:3, :] = wpos_ref[...]
    table_ref[3:4, :] = core * core
    table_ref[4:7, :] = wgam_ref[...]


def prologue(dust_pos, dust_vel, dust_tau, dest, counts, wake_pos, wake_gamma, wake_core):
    per_device = dust_tau.shape[0]
    regions = lax.axis_size("region")
    capacity = 2 * per_device // regions
    wake_count = wake_core.shape[0]
    vmem = pl.BlockSpec(memory_space=pltpu.VMEM)
    return pl.pallas_call(
        prologue_kernel,
        out_shape=tuple(
            [jax.ShapeDtypeStruct((8, capacity), jnp.float32)] * regions
            + [jax.ShapeDtypeStruct((7, wake_count), jnp.float32)]
        ),
        in_specs=[pl.BlockSpec(memory_space=pltpu.SMEM)] + [vmem] * 7,
        out_specs=tuple([vmem] * (regions + 1)),
        scratch_shapes=[pltpu.VMEM((24, per_device), jnp.float32)],
    )(
        counts, dust_pos, dust_vel, dust_tau.reshape(1, per_device), dest.reshape(1, per_device),
        wake_pos, wake_gamma, wake_core.reshape(1, wake_count),
    )


def exchange_slots(by_offset):
    regions = len(by_offset)
    rows, capacity = by_offset[0].shape
    region = lax.axis_index("region")
    if regions > 8:
        by_offset = jnp.stack(by_offset)
        back = (jnp.arange(regions, dtype=jnp.int32) - region) % regions
        blocks = jnp.take(by_offset, back, axis=0)
        arrived = lax.all_to_all(blocks, "region", split_axis=0, concat_axis=0, tiled=True)
        return arrived.transpose(1, 0, 2).reshape(rows, regions * capacity)
    by_shift = [by_offset[0]]
    for shift in range(1, regions):
        pairs = [(i, (i + shift) % regions) for i in range(regions)]
        by_shift.append(lax.ppermute(by_offset[shift], "region", pairs))
    placed = []
    for source in range(regions):
        shift = (region - source) % regions
        block = by_shift[0]
        for other in range(1, regions):
            block = jnp.where(shift == other, by_shift[other], block)
        placed.append(block)
    return jnp.concatenate(placed, axis=1)


def wake_tables(gathered):
    place = gathered[0:3]
    gamma = gathered[4:7]
    return jnp.concatenate([gathered, cross_rows(gamma, place)], axis=0)


def body(dust_pos, dust_vel, dust_tau, dest, counts, wake_pos, wake_gamma, wake_core):
    *outgoing, wake_table = prologue(
        dust_pos, dust_vel, dust_tau, dest, counts, wake_pos, wake_gamma, wake_core
    )
    outgoing, wake_table = lax.optimization_barrier((tuple(outgoing), wake_table))
    arrived = exchange_slots(outgoing)
    region_table = wake_tables(lax.all_gather(wake_table, "narrow", axis=1, tiled=True))
    points = arrived[0:3]
    raw_sums = raw_terms(points, region_table)
    return advance(arrived, raw_sums)


def solution(mesh):
    in_specs = (
        P(None, ("region", "narrow")),
        P(None, ("region", "narrow")),
        P(("region", "narrow")),
        P(("region", "narrow"), None),
        P(("region", "narrow")),
        P(None, ("region", "narrow")),
        P(None, ("region", "narrow")),
        P(("region", "narrow")),
    )
    out_specs = P(None, ("region", "narrow"))
    return jax.shard_map(body, mesh=mesh, in_specs=in_specs, out_specs=out_specs, check_vma=False)
```

```python
import functools
import math

import jax
import jax.numpy as jnp
from jax import lax
from jax.experimental import pallas as pl
from jax.experimental.pallas import tpu as pltpu
from jax.sharding import PartitionSpec as P

step_size = 0.1
gravity = 1.0


def cross_rows(first, second):
    return jnp.stack(
        [
            first[1] * second[2] - first[2] * second[1],
            first[2] * second[0] - first[0] * second[2],
            first[0] * second[1] - first[1] * second[0],
        ]
    )


def raw_terms(points, wake_table):
    point_count = points.shape[1]
    wake_count = wake_table.shape[1]
    wake_width = math.gcd(wake_count, 8192)
    scaled_place = wake_table[0:3]
    wake_offset = wake_table[3]
    tables = wake_table[4:10]
    place_blocks = scaled_place.reshape(3, wake_count // wake_width, wake_width).transpose(1, 0, 2)
    table_blocks = tables.reshape(6, wake_count // wake_width, wake_width).transpose(1, 0, 2)
    core_blocks = wake_offset.reshape(wake_count // wake_width, wake_width)
    point_blocks = points.reshape(3, point_count // point_count, point_count).transpose(1, 0, 2)

    def one_block(point_group):
        point_sq = (
            point_group[0] * point_group[0]
            + point_group[1] * point_group[1]
            + point_group[2] * point_group[2]
        )

        def accumulate(running, parts):
            scaled_place, table_part, offset_part = parts
            distance_sq = (
                (offset_part[:, None] + point_sq[None, :])
                + scaled_place[0][:, None] * point_group[0][None, :]
                + scaled_place[1][:, None] * point_group[1][None, :]
                + scaled_place[2][:, None] * point_group[2][None, :]
            )
            inverse_root = lax.rsqrt(distance_sq)
            kernel = inverse_root * inverse_root * inverse_root
            product = lax.dot_general(
                table_part, kernel, (((1,), (0,)), ((), ())), precision=lax.Precision.HIGH
            )
            return (running + product, None)

        total, _ = lax.scan(
            accumulate,
            jnp.zeros((6, point_count), jnp.float32),
            (place_blocks, table_blocks, core_blocks),
        )
        return total

    result = lax.map(one_block, point_blocks)
    return result.transpose(1, 0, 2).reshape(6, point_count)


def advance(arrived, raw_sums):
    points = arrived[0:3]
    velocity = arrived[3:6]
    live_flag = arrived[7]
    wind = (cross_rows(raw_sums[0:3], points) - raw_sums[3:6]) / (4.0 * math.pi)
    safe_tau = jnp.where(live_flag > 0.5, arrived[6], 1.0)
    rate = step_size / safe_tau
    upward = jnp.array([0.0, 0.0, 1.0], jnp.float32)[:, None]
    new_velocity = (velocity + rate[None, :] * wind - step_size * gravity * upward) / (
        1.0 + rate[None, :]
    )
    new_place = points + step_size * new_velocity
    return jnp.concatenate([new_place, new_velocity], axis=0) * live_flag[None, :]


def prologue_kernel(
    count_ref, pos_ref, vel_ref, tau_ref, dest_ref, wpos_ref, wgam_ref, wcore_ref, *refs
):
    out_refs = refs[:-2]
    table_ref, split_ref = refs[-2:]
    regions = len(out_refs)
    capacity = out_refs[0].shape[1]
    per_device = dest_ref.shape[1]
    target = dest_ref[...]
    region_id = lax.broadcasted_iota(jnp.int32, (regions, per_device), 0)
    onehot = (target == region_id).astype(jnp.float32)
    row = lax.broadcasted_iota(jnp.int32, (per_device, per_device), 0)
    col = lax.broadcasted_iota(jnp.int32, (per_device, per_device), 1)
    upper = (row < col).astype(jnp.bfloat16)
    before = jnp.dot(onehot.astype(jnp.bfloat16), upper, preferred_element_type=jnp.float32)
    slot_rank = jnp.sum(before * onehot, axis=0, keepdims=True).astype(jnp.int32)
    column = target * capacity + slot_rank
    live = lax.broadcasted_iota(jnp.int32, (1, per_device), 1) < count_ref[0]
    state = jnp.concatenate(
        [pos_ref[...], vel_ref[...], tau_ref[...], jnp.ones((1, per_device), jnp.float32)], axis=0
    )
    high = state.astype(jnp.bfloat16).astype(jnp.float32)
    rest = state - high
    middle = rest.astype(jnp.bfloat16).astype(jnp.float32)
    split_ref[0:8, :] = high
    split_ref[8:16, :] = middle
    split_ref[16:24, :] = rest - middle
    split = split_ref[...].astype(jnp.bfloat16)
    region = lax.axis_index("region")
    for shift, out_ref in enumerate(out_refs):
        dest_region = (region + shift) % regions
        slot_id = lax.broadcasted_iota(jnp.int32, (capacity, per_device), 0) + dest_region * capacity
        placing = ((column == slot_id) & live).astype(jnp.bfloat16)
        parts = lax.dot_general(
            split, placing, (((1,), (1,)), ((), ())), preferred_element_type=jnp.float32
        )
        out_ref[...] = (parts[0:8] + parts[8:16]) + parts[16:24]
    core = wcore_ref[...]
    place = wpos_ref[...]
    table_ref[0:3, :] = -2.0 * place
    table_ref[3:4, :] = (
        place[0:1] * place[0:1] + place[1:2] * place[1:2] + place[2:3] * place[2:3] + core * core
    )
    table_ref[4:7, :] = wgam_ref[...]


def prologue(dust_pos, dust_vel, dust_tau, dest, counts, wake_pos, wake_gamma, wake_core):
    per_device = dust_tau.shape[0]
    regions = lax.axis_size("region")
    capacity = 2 * per_device // regions
    wake_count = wake_core.shape[0]
    vmem = pl.BlockSpec(memory_space=pltpu.VMEM)
    return pl.pallas_call(
        prologue_kernel,
        out_shape=tuple(
            [jax.ShapeDtypeStruct((8, capacity), jnp.float32)] * regions
            + [jax.ShapeDtypeStruct((7, wake_count), jnp.float32)]
        ),
        in_specs=[pl.BlockSpec(memory_space=pltpu.SMEM)] + [vmem] * 7,
        out_specs=tuple([vmem] * (regions + 1)),
        scratch_shapes=[pltpu.VMEM((24, per_device), jnp.float32)],
    )(
        counts, dust_pos, dust_vel, dust_tau.reshape(1, per_device), dest.reshape(1, per_device),
        wake_pos, wake_gamma, wake_core.reshape(1, wake_count),
    )


def exchange_slots(by_offset):
    regions = len(by_offset)
    rows, capacity = by_offset[0].shape
    region = lax.axis_index("region")
    if regions > 8:
        by_offset = jnp.stack(by_offset)
        back = (jnp.arange(regions, dtype=jnp.int32) - region) % regions
        blocks = jnp.take(by_offset, back, axis=0)
        arrived = lax.all_to_all(blocks, "region", split_axis=0, concat_axis=0, tiled=True)
        return arrived.transpose(1, 0, 2).reshape(rows, regions * capacity)
    by_shift = [by_offset[0]]
    for shift in range(1, regions):
        pairs = [(i, (i + shift) % regions) for i in range(regions)]
        by_shift.append(lax.ppermute(by_offset[shift], "region", pairs))
    placed = []
    for source in range(regions):
        shift = (region - source) % regions
        block = by_shift[0]
        for other in range(1, regions):
            block = jnp.where(shift == other, by_shift[other], block)
        placed.append(block)
    return jnp.concatenate(placed, axis=1)


def wake_tables(gathered):
    scaled_place = gathered[0:3]
    gamma = gathered[4:7]
    return jnp.concatenate([gathered, -0.5 * cross_rows(gamma, scaled_place)], axis=0)


def body(dust_pos, dust_vel, dust_tau, dest, counts, wake_pos, wake_gamma, wake_core):
    *outgoing, wake_table = prologue(
        dust_pos, dust_vel, dust_tau, dest, counts, wake_pos, wake_gamma, wake_core
    )
    outgoing, wake_table = lax.optimization_barrier((tuple(outgoing), wake_table))
    arrived = exchange_slots(outgoing)
    region_table = wake_tables(lax.all_gather(wake_table, "narrow", axis=1, tiled=True))
    points = arrived[0:3]
    raw_sums = raw_terms(points, region_table)
    return advance(arrived, raw_sums)


def solution(mesh):
    in_specs = (
        P(None, ("region", "narrow")),
        P(None, ("region", "narrow")),
        P(("region", "narrow")),
        P(("region", "narrow"), None),
        P(("region", "narrow")),
        P(None, ("region", "narrow")),
        P(None, ("region", "narrow")),
        P(("region", "narrow")),
    )
    out_specs = P(None, ("region", "narrow"))
    return jax.shard_map(body, mesh=mesh, in_specs=in_specs, out_specs=out_specs, check_vma=False)
```

```python
import functools
import math

import jax
import jax.numpy as jnp
from jax import lax
from jax.experimental import pallas as pl
from jax.experimental.pallas import tpu as pltpu
from jax.sharding import PartitionSpec as P

step_size = 0.1
gravity = 1.0


def cross_rows(first, second):
    return jnp.stack(
        [
            first[1] * second[2] - first[2] * second[1],
            first[2] * second[0] - first[0] * second[2],
            first[0] * second[1] - first[1] * second[0],
        ]
    )


def raw_terms(points, wake_table):
    point_count = points.shape[1]
    wake_count = wake_table.shape[1]
    wake_width = math.gcd(wake_count, 8192)
    scaled_place = wake_table[0:3]
    wake_offset = wake_table[3]
    tables = wake_table[4:10]
    place_blocks = scaled_place.reshape(3, wake_count // wake_width, wake_width).transpose(1, 0, 2)
    table_blocks = tables.reshape(6, wake_count // wake_width, wake_width).transpose(1, 0, 2)
    core_blocks = wake_offset.reshape(wake_count // wake_width, wake_width)
    point_blocks = points.reshape(3, point_count // point_count, point_count).transpose(1, 0, 2)

    def one_block(point_group):
        point_sq = (
            point_group[0] * point_group[0]
            + point_group[1] * point_group[1]
            + point_group[2] * point_group[2]
        )

        def accumulate(running, parts):
            scaled_place, table_part, offset_part = parts
            distance_sq = (
                (offset_part[:, None] + point_sq[None, :])
                + scaled_place[0][:, None] * point_group[0][None, :]
                + scaled_place[1][:, None] * point_group[1][None, :]
                + scaled_place[2][:, None] * point_group[2][None, :]
            )
            inverse_root = lax.rsqrt(distance_sq)
            kernel = inverse_root * inverse_root * inverse_root
            product = lax.dot_general(
                table_part, kernel, (((1,), (0,)), ((), ())), precision=lax.Precision.HIGH
            )
            return (running + product, None)

        total, _ = lax.scan(
            accumulate,
            jnp.zeros((6, point_count), jnp.float32),
            (place_blocks, table_blocks, core_blocks),
        )
        return total

    result = lax.map(one_block, point_blocks)
    return result.transpose(1, 0, 2).reshape(6, point_count)


def advance(arrived, raw_sums):
    points = arrived[0:3]
    velocity = arrived[3:6]
    live_flag = arrived[7]
    wind = (cross_rows(raw_sums[0:3], points) - raw_sums[3:6]) / (4.0 * math.pi)
    safe_tau = jnp.where(live_flag > 0.5, arrived[6], 1.0)
    rate = step_size / safe_tau
    upward = jnp.array([0.0, 0.0, 1.0], jnp.float32)[:, None]
    new_velocity = (velocity + rate[None, :] * wind - step_size * gravity * upward) / (
        1.0 + rate[None, :]
    )
    new_place = points + step_size * new_velocity
    return jnp.concatenate([new_place, new_velocity], axis=0) * live_flag[None, :]


def prologue_kernel(
    count_ref, pos_ref, vel_ref, tau_ref, dest_ref, wpos_ref, wgam_ref, wcore_ref, *refs
):
    out_refs = refs[:-2]
    table_ref, split_ref = refs[-2:]
    regions = len(out_refs)
    capacity = out_refs[0].shape[1]
    per_device = dest_ref.shape[1]
    target = dest_ref[...]
    region_id = lax.broadcasted_iota(jnp.int32, (regions, per_device), 0)
    onehot = (target == region_id).astype(jnp.float32)
    row = lax.broadcasted_iota(jnp.int32, (per_device, per_device), 0)
    col = lax.broadcasted_iota(jnp.int32, (per_device, per_device), 1)
    upper = (row < col).astype(jnp.bfloat16)
    before = jnp.dot(onehot.astype(jnp.bfloat16), upper, preferred_element_type=jnp.float32)
    slot_rank = jnp.sum(before * onehot, axis=0, keepdims=True).astype(jnp.int32)
    column = target * capacity + slot_rank
    live = lax.broadcasted_iota(jnp.int32, (1, per_device), 1) < count_ref[0]
    state = jnp.concatenate(
        [pos_ref[...], vel_ref[...], tau_ref[...], jnp.ones((1, per_device), jnp.float32)], axis=0
    )
    high = state.astype(jnp.bfloat16).astype(jnp.float32)
    rest = state - high
    middle = rest.astype(jnp.bfloat16).astype(jnp.float32)
    split_ref[0:8, :] = high
    split_ref[8:16, :] = middle
    split_ref[16:24, :] = rest - middle
    split = split_ref[...].astype(jnp.bfloat16)
    region = lax.axis_index("region")
    for shift, out_ref in enumerate(out_refs):
        dest_region = (region + shift) % regions
        slot_id = lax.broadcasted_iota(jnp.int32, (capacity, per_device), 0) + dest_region * capacity
        placing = ((column == slot_id) & live).astype(jnp.bfloat16)
        parts = lax.dot_general(
            split, placing, (((1,), (1,)), ((), ())), preferred_element_type=jnp.float32
        )
        out_ref[...] = (parts[0:8] + parts[8:16]) + parts[16:24]
    core = wcore_ref[...]
    place = wpos_ref[...]
    table_ref[0:3, :] = -2.0 * place
    table_ref[3:4, :] = (
        place[0:1] * place[0:1] + place[1:2] * place[1:2] + place[2:3] * place[2:3] + core * core
    )
    table_ref[4:7, :] = wgam_ref[...]


def prologue(dust_pos, dust_vel, dust_tau, dest, counts, wake_pos, wake_gamma, wake_core):
    per_device = dust_tau.shape[0]
    regions = lax.axis_size("region")
    capacity = 2 * per_device // regions
    wake_count = wake_core.shape[0]
    vmem = pl.BlockSpec(memory_space=pltpu.VMEM)
    return pl.pallas_call(
        prologue_kernel,
        out_shape=tuple(
            [jax.ShapeDtypeStruct((8, capacity), jnp.float32)] * regions
            + [jax.ShapeDtypeStruct((7, wake_count), jnp.float32)]
        ),
        in_specs=[pl.BlockSpec(memory_space=pltpu.SMEM)] + [vmem] * 7,
        out_specs=tuple([vmem] * (regions + 1)),
        scratch_shapes=[pltpu.VMEM((24, per_device), jnp.float32)],
    )(
        counts, dust_pos, dust_vel, dust_tau.reshape(1, per_device), dest.reshape(1, per_device),
        wake_pos, wake_gamma, wake_core.reshape(1, wake_count),
    )


def exchange_slots(by_offset):
    regions = len(by_offset)
    rows, capacity = by_offset[0].shape
    region = lax.axis_index("region")
    if regions > 8:
        by_offset = jnp.stack(by_offset)
        back = (jnp.arange(regions, dtype=jnp.int32) - region) % regions
        blocks = jnp.take(by_offset, back, axis=0)
        arrived = lax.all_to_all(blocks, "region", split_axis=0, concat_axis=0, tiled=True)
        return arrived.transpose(1, 0, 2).reshape(rows, regions * capacity)
    by_shift = [by_offset[0]]
    for shift in range(1, regions):
        pairs = [(i, (i + shift) % regions) for i in range(regions)]
        by_shift.append(lax.ppermute(by_offset[shift], "region", pairs))
    placed = []
    for source in range(regions):
        shift = (region - source) % regions
        block = by_shift[0]
        for other in range(1, regions):
            block = jnp.where(shift == other, by_shift[other], block)
        placed.append(block)
    return jnp.concatenate(placed, axis=1)


def wake_tables(gathered):
    scaled_place = gathered[0:3]
    gamma = gathered[4:7]
    return jnp.concatenate([gathered, -0.5 * cross_rows(gamma, scaled_place)], axis=0)


def body(dust_pos, dust_vel, dust_tau, dest, counts, wake_pos, wake_gamma, wake_core):
    *outgoing, wake_table = prologue(
        dust_pos, dust_vel, dust_tau, dest, counts, wake_pos, wake_gamma, wake_core
    )
    gathered = lax.all_gather(wake_table, "narrow", axis=1, tiled=True)
    outgoing, gathered = lax.optimization_barrier((tuple(outgoing), gathered))
    arrived = exchange_slots(outgoing)
    region_table = wake_tables(gathered)
    points = arrived[0:3]
    raw_sums = raw_terms(points, region_table)
    return advance(arrived, raw_sums)


def solution(mesh):
    in_specs = (
        P(None, ("region", "narrow")),
        P(None, ("region", "narrow")),
        P(("region", "narrow")),
        P(("region", "narrow"), None),
        P(("region", "narrow")),
        P(None, ("region", "narrow")),
        P(None, ("region", "narrow")),
        P(("region", "narrow")),
    )
    out_specs = P(None, ("region", "narrow"))
    return jax.shard_map(body, mesh=mesh, in_specs=in_specs, out_specs=out_specs, check_vma=False)
```

```python
import functools
import math

import jax
import jax.numpy as jnp
from jax import lax
from jax.experimental import pallas as pl
from jax.experimental.pallas import tpu as pltpu
from jax.sharding import PartitionSpec as P

step_size = 0.1
gravity = 1.0


def cross_rows(first, second):
    return jnp.stack(
        [
            first[1] * second[2] - first[2] * second[1],
            first[2] * second[0] - first[0] * second[2],
            first[0] * second[1] - first[1] * second[0],
        ]
    )


def raw_terms(points, wake_table):
    point_count = points.shape[1]
    wake_count = wake_table.shape[1]
    wake_width = math.gcd(wake_count, 8192)
    scaled_place = wake_table[0:3]
    wake_offset = wake_table[3]
    tables = wake_table[4:10]
    place_blocks = scaled_place.reshape(3, wake_count // wake_width, wake_width).transpose(1, 0, 2)
    table_blocks = tables.reshape(6, wake_count // wake_width, wake_width).transpose(1, 0, 2)
    core_blocks = wake_offset.reshape(wake_count // wake_width, wake_width)
    point_blocks = points.reshape(3, point_count // point_count, point_count).transpose(1, 0, 2)

    def one_block(point_group):
        point_sq = (
            point_group[0] * point_group[0]
            + point_group[1] * point_group[1]
            + point_group[2] * point_group[2]
        )

        def accumulate(running, parts):
            scaled_place, table_part, offset_part = parts
            distance_sq = (
                (offset_part[:, None] + point_sq[None, :])
                + scaled_place[0][:, None] * point_group[0][None, :]
                + scaled_place[1][:, None] * point_group[1][None, :]
                + scaled_place[2][:, None] * point_group[2][None, :]
            )
            inverse_root = lax.rsqrt(distance_sq)
            kernel = inverse_root * inverse_root * inverse_root
            product = lax.dot_general(
                table_part, kernel, (((1,), (0,)), ((), ())), precision=lax.Precision.HIGH
            )
            return (running + product, None)

        total, _ = lax.scan(
            accumulate,
            jnp.zeros((6, point_count), jnp.float32),
            (place_blocks, table_blocks, core_blocks),
        )
        return total

    result = lax.map(one_block, point_blocks)
    return result.transpose(1, 0, 2).reshape(6, point_count)


def advance(arrived, raw_sums):
    points = arrived[0:3]
    velocity = arrived[3:6]
    live_flag = arrived[7]
    swirl = cross_rows(raw_sums[0:3], points) - raw_sums[3:6]
    safe_tau = jnp.where(live_flag > 0.5, arrived[6], 1.0)
    rate = step_size / safe_tau
    drive = rate * (1.0 / (4.0 * math.pi))
    damping = 1.0 / (1.0 + rate)
    upward = jnp.array([0.0, 0.0, 1.0], jnp.float32)[:, None]
    new_velocity = (velocity + drive[None, :] * swirl - step_size * gravity * upward) * damping[
        None, :
    ]
    new_place = points + step_size * new_velocity
    return jnp.concatenate([new_place, new_velocity], axis=0) * live_flag[None, :]


def prologue_kernel(
    count_ref, pos_ref, vel_ref, tau_ref, dest_ref, wpos_ref, wgam_ref, wcore_ref, *refs
):
    out_refs = refs[:-2]
    table_ref, split_ref = refs[-2:]
    regions = len(out_refs)
    capacity = out_refs[0].shape[1]
    per_device = dest_ref.shape[1]
    target = dest_ref[...]
    region_id = lax.broadcasted_iota(jnp.int32, (regions, per_device), 0)
    onehot = (target == region_id).astype(jnp.float32)
    row = lax.broadcasted_iota(jnp.int32, (per_device, per_device), 0)
    col = lax.broadcasted_iota(jnp.int32, (per_device, per_device), 1)
    upper = (row < col).astype(jnp.bfloat16)
    before = jnp.dot(onehot.astype(jnp.bfloat16), upper, preferred_element_type=jnp.float32)
    slot_rank = jnp.sum(before * onehot, axis=0, keepdims=True).astype(jnp.int32)
    column = target * capacity + slot_rank
    live = lax.broadcasted_iota(jnp.int32, (1, per_device), 1) < count_ref[0]
    state = jnp.concatenate(
        [pos_ref[...], vel_ref[...], tau_ref[...], jnp.ones((1, per_device), jnp.float32)], axis=0
    )
    high = state.astype(jnp.bfloat16).astype(jnp.float32)
    rest = state - high
    middle = rest.astype(jnp.bfloat16).astype(jnp.float32)
    split_ref[0:8, :] = high
    split_ref[8:16, :] = middle
    split_ref[16:24, :] = rest - middle
    split = split_ref[...].astype(jnp.bfloat16)
    region = lax.axis_index("region")
    for shift, out_ref in enumerate(out_refs):
        dest_region = (region + shift) % regions
        slot_id = lax.broadcasted_iota(jnp.int32, (capacity, per_device), 0) + dest_region * capacity
        placing = ((column == slot_id) & live).astype(jnp.bfloat16)
        parts = lax.dot_general(
            split, placing, (((1,), (1,)), ((), ())), preferred_element_type=jnp.float32
        )
        out_ref[...] = (parts[0:8] + parts[8:16]) + parts[16:24]
    core = wcore_ref[...]
    place = wpos_ref[...]
    table_ref[0:3, :] = -2.0 * place
    table_ref[3:4, :] = (
        place[0:1] * place[0:1] + place[1:2] * place[1:2] + place[2:3] * place[2:3] + core * core
    )
    table_ref[4:7, :] = wgam_ref[...]


def prologue(dust_pos, dust_vel, dust_tau, dest, counts, wake_pos, wake_gamma, wake_core):
    per_device = dust_tau.shape[0]
    regions = lax.axis_size("region")
    capacity = 2 * per_device // regions
    wake_count = wake_core.shape[0]
    vmem = pl.BlockSpec(memory_space=pltpu.VMEM)
    return pl.pallas_call(
        prologue_kernel,
        out_shape=tuple(
            [jax.ShapeDtypeStruct((8, capacity), jnp.float32)] * regions
            + [jax.ShapeDtypeStruct((7, wake_count), jnp.float32)]
        ),
        in_specs=[pl.BlockSpec(memory_space=pltpu.SMEM)] + [vmem] * 7,
        out_specs=tuple([vmem] * (regions + 1)),
        scratch_shapes=[pltpu.VMEM((24, per_device), jnp.float32)],
    )(
        counts, dust_pos, dust_vel, dust_tau.reshape(1, per_device), dest.reshape(1, per_device),
        wake_pos, wake_gamma, wake_core.reshape(1, wake_count),
    )


def exchange_slots(by_offset):
    regions = len(by_offset)
    rows, capacity = by_offset[0].shape
    region = lax.axis_index("region")
    if regions > 8:
        by_offset = jnp.stack(by_offset)
        back = (jnp.arange(regions, dtype=jnp.int32) - region) % regions
        blocks = jnp.take(by_offset, back, axis=0)
        arrived = lax.all_to_all(blocks, "region", split_axis=0, concat_axis=0, tiled=True)
        return arrived.transpose(1, 0, 2).reshape(rows, regions * capacity)
    by_shift = [by_offset[0]]
    for shift in range(1, regions):
        pairs = [(i, (i + shift) % regions) for i in range(regions)]
        by_shift.append(lax.ppermute(by_offset[shift], "region", pairs))
    placed = []
    for source in range(regions):
        shift = (region - source) % regions
        block = by_shift[0]
        for other in range(1, regions):
            block = jnp.where(shift == other, by_shift[other], block)
        placed.append(block)
    return jnp.concatenate(placed, axis=1)


def wake_tables(gathered):
    scaled_place = gathered[0:3]
    gamma = gathered[4:7]
    return jnp.concatenate([gathered, -0.5 * cross_rows(gamma, scaled_place)], axis=0)


def body(dust_pos, dust_vel, dust_tau, dest, counts, wake_pos, wake_gamma, wake_core):
    *outgoing, wake_table = prologue(
        dust_pos, dust_vel, dust_tau, dest, counts, wake_pos, wake_gamma, wake_core
    )
    outgoing, wake_table = lax.optimization_barrier((tuple(outgoing), wake_table))
    arrived = exchange_slots(outgoing)
    region_table = wake_tables(lax.all_gather(wake_table, "narrow", axis=1, tiled=True))
    points = arrived[0:3]
    raw_sums = raw_terms(points, region_table)
    return advance(arrived, raw_sums)


def solution(mesh):
    in_specs = (
        P(None, ("region", "narrow")),
        P(None, ("region", "narrow")),
        P(("region", "narrow")),
        P(("region", "narrow"), None),
        P(("region", "narrow")),
        P(None, ("region", "narrow")),
        P(None, ("region", "narrow")),
        P(("region", "narrow")),
    )
    out_specs = P(None, ("region", "narrow"))
    return jax.shard_map(body, mesh=mesh, in_specs=in_specs, out_specs=out_specs, check_vma=False)
```

```python
import functools
import math

import jax
import jax.numpy as jnp
from jax import lax
from jax.experimental import pallas as pl
from jax.experimental.pallas import tpu as pltpu
from jax.sharding import PartitionSpec as P

step_size = 0.1
gravity = 1.0


def cross_rows(first, second):
    return jnp.stack(
        [
            first[1] * second[2] - first[2] * second[1],
            first[2] * second[0] - first[0] * second[2],
            first[0] * second[1] - first[1] * second[0],
        ]
    )


def raw_terms(points, wake_table):
    point_count = points.shape[1]
    wake_count = wake_table.shape[1]
    wake_width = math.gcd(wake_count, 8192)
    scaled_place = wake_table[0:3]
    wake_offset = wake_table[3]
    tables = wake_table[4:10]
    columns = lax.optimization_barrier(jnp.stack([scaled_place[0], scaled_place[1], scaled_place[2], wake_offset], axis=1))
    scaled_place = columns[:, 0:3].T
    wake_offset = columns[:, 3]
    place_blocks = scaled_place.reshape(3, wake_count // wake_width, wake_width).transpose(1, 0, 2)
    table_blocks = tables.reshape(6, wake_count // wake_width, wake_width).transpose(1, 0, 2)
    core_blocks = wake_offset.reshape(wake_count // wake_width, wake_width)
    point_blocks = points.reshape(3, point_count // point_count, point_count).transpose(1, 0, 2)

    def one_block(point_group):
        point_sq = (
            point_group[0] * point_group[0]
            + point_group[1] * point_group[1]
            + point_group[2] * point_group[2]
        )

        def accumulate(running, parts):
            scaled_place, table_part, offset_part = parts
            distance_sq = (
                (offset_part[:, None] + point_sq[None, :])
                + scaled_place[0][:, None] * point_group[0][None, :]
                + scaled_place[1][:, None] * point_group[1][None, :]
                + scaled_place[2][:, None] * point_group[2][None, :]
            )
            inverse_root = lax.rsqrt(distance_sq)
            kernel = inverse_root * inverse_root * inverse_root
            product = lax.dot_general(
                table_part, kernel, (((1,), (0,)), ((), ())), precision=lax.Precision.HIGH
            )
            return (running + product, None)

        total, _ = lax.scan(
            accumulate,
            jnp.zeros((6, point_count), jnp.float32),
            (place_blocks, table_blocks, core_blocks),
        )
        return total

    result = lax.map(one_block, point_blocks)
    return result.transpose(1, 0, 2).reshape(6, point_count)


def advance(arrived, raw_sums):
    points = arrived[0:3]
    velocity = arrived[3:6]
    live_flag = arrived[7]
    swirl = cross_rows(raw_sums[0:3], points) - raw_sums[3:6]
    safe_tau = jnp.where(live_flag > 0.5, arrived[6], 1.0)
    rate = step_size / safe_tau
    drive = rate * (1.0 / (4.0 * math.pi))
    damping = 1.0 / (1.0 + rate)
    upward = jnp.array([0.0, 0.0, 1.0], jnp.float32)[:, None]
    new_velocity = (velocity + drive[None, :] * swirl - step_size * gravity * upward) * damping[
        None, :
    ]
    new_place = points + step_size * new_velocity
    return jnp.concatenate([new_place, new_velocity], axis=0) * live_flag[None, :]


def prologue_kernel(
    count_ref, pos_ref, vel_ref, tau_ref, dest_ref, wpos_ref, wgam_ref, wcore_ref, *refs
):
    out_refs = refs[:-2]
    table_ref, split_ref = refs[-2:]
    regions = len(out_refs)
    capacity = out_refs[0].shape[1]
    per_device = dest_ref.shape[1]
    target = dest_ref[...]
    region_id = lax.broadcasted_iota(jnp.int32, (regions, per_device), 0)
    onehot = (target == region_id).astype(jnp.float32)
    row = lax.broadcasted_iota(jnp.int32, (per_device, per_device), 0)
    col = lax.broadcasted_iota(jnp.int32, (per_device, per_device), 1)
    upper = (row < col).astype(jnp.bfloat16)
    before = jnp.dot(onehot.astype(jnp.bfloat16), upper, preferred_element_type=jnp.float32)
    slot_rank = jnp.sum(before * onehot, axis=0, keepdims=True).astype(jnp.int32)
    column = target * capacity + slot_rank
    live = lax.broadcasted_iota(jnp.int32, (1, per_device), 1) < count_ref[0]
    state = jnp.concatenate(
        [pos_ref[...], vel_ref[...], tau_ref[...], jnp.ones((1, per_device), jnp.float32)], axis=0
    )
    high = state.astype(jnp.bfloat16).astype(jnp.float32)
    rest = state - high
    middle = rest.astype(jnp.bfloat16).astype(jnp.float32)
    split_ref[0:8, :] = high
    split_ref[8:16, :] = middle
    split_ref[16:24, :] = rest - middle
    split = split_ref[...].astype(jnp.bfloat16)
    region = lax.axis_index("region")
    for shift, out_ref in enumerate(out_refs):
        dest_region = (region + shift) % regions
        slot_id = lax.broadcasted_iota(jnp.int32, (capacity, per_device), 0) + dest_region * capacity
        placing = ((column == slot_id) & live).astype(jnp.bfloat16)
        parts = lax.dot_general(
            split, placing, (((1,), (1,)), ((), ())), preferred_element_type=jnp.float32
        )
        out_ref[...] = (parts[0:8] + parts[8:16]) + parts[16:24]
    core = wcore_ref[...]
    place = wpos_ref[...]
    table_ref[0:3, :] = -2.0 * place
    table_ref[3:4, :] = (
        place[0:1] * place[0:1] + place[1:2] * place[1:2] + place[2:3] * place[2:3] + core * core
    )
    table_ref[4:7, :] = wgam_ref[...]


def prologue(dust_pos, dust_vel, dust_tau, dest, counts, wake_pos, wake_gamma, wake_core):
    per_device = dust_tau.shape[0]
    regions = lax.axis_size("region")
    capacity = 2 * per_device // regions
    wake_count = wake_core.shape[0]
    vmem = pl.BlockSpec(memory_space=pltpu.VMEM)
    return pl.pallas_call(
        prologue_kernel,
        out_shape=tuple(
            [jax.ShapeDtypeStruct((8, capacity), jnp.float32)] * regions
            + [jax.ShapeDtypeStruct((7, wake_count), jnp.float32)]
        ),
        in_specs=[pl.BlockSpec(memory_space=pltpu.SMEM)] + [vmem] * 7,
        out_specs=tuple([vmem] * (regions + 1)),
        scratch_shapes=[pltpu.VMEM((24, per_device), jnp.float32)],
    )(
        counts, dust_pos, dust_vel, dust_tau.reshape(1, per_device), dest.reshape(1, per_device),
        wake_pos, wake_gamma, wake_core.reshape(1, wake_count),
    )


def exchange_slots(by_offset):
    regions = len(by_offset)
    rows, capacity = by_offset[0].shape
    region = lax.axis_index("region")
    if regions > 8:
        by_offset = jnp.stack(by_offset)
        back = (jnp.arange(regions, dtype=jnp.int32) - region) % regions
        blocks = jnp.take(by_offset, back, axis=0)
        arrived = lax.all_to_all(blocks, "region", split_axis=0, concat_axis=0, tiled=True)
        return arrived.transpose(1, 0, 2).reshape(rows, regions * capacity)
    by_shift = [by_offset[0]]
    for shift in range(1, regions):
        pairs = [(i, (i + shift) % regions) for i in range(regions)]
        by_shift.append(lax.ppermute(by_offset[shift], "region", pairs))
    placed = []
    for source in range(regions):
        shift = (region - source) % regions
        block = by_shift[0]
        for other in range(1, regions):
            block = jnp.where(shift == other, by_shift[other], block)
        placed.append(block)
    return jnp.concatenate(placed, axis=1)


def wake_tables(gathered):
    scaled_place = gathered[0:3]
    gamma = gathered[4:7]
    return jnp.concatenate([gathered, -0.5 * cross_rows(gamma, scaled_place)], axis=0)


def body(dust_pos, dust_vel, dust_tau, dest, counts, wake_pos, wake_gamma, wake_core):
    *outgoing, wake_table = prologue(
        dust_pos, dust_vel, dust_tau, dest, counts, wake_pos, wake_gamma, wake_core
    )
    outgoing, wake_table = lax.optimization_barrier((tuple(outgoing), wake_table))
    arrived = exchange_slots(outgoing)
    region_table = wake_tables(lax.all_gather(wake_table, "narrow", axis=1, tiled=True))
    points = arrived[0:3]
    raw_sums = raw_terms(points, region_table)
    return advance(arrived, raw_sums)


def solution(mesh):
    in_specs = (
        P(None, ("region", "narrow")),
        P(None, ("region", "narrow")),
        P(("region", "narrow")),
        P(("region", "narrow"), None),
        P(("region", "narrow")),
        P(None, ("region", "narrow")),
        P(None, ("region", "narrow")),
        P(("region", "narrow")),
    )
    out_specs = P(None, ("region", "narrow"))
    return jax.shard_map(body, mesh=mesh, in_specs=in_specs, out_specs=out_specs, check_vma=False)
```
